128 devices in a mesh: section: 8 (over y, core), seq: 16 (over z, x).
Axes of the slice: x: 4, y: 4, z: 4, core: 2. Of those that a mesh axis runs over, the one named last changes fastest.
Arguments:
- hidden: bfloat16 [2, 2048, 4096], P(None, 'seq'), may hold values from -6 to 6
- queries: bfloat16 [8, 2, 2048, 4096], P('section', None, 'seq'), may hold values from -6 to 6
- gain: float32 [8, 4096], P('section'), may hold values from 0.5 to 2
- key_weight: bfloat16 [8, 4096, 512], P('section'), may hold values from -1 to 1
- value_weight: bfloat16 [8, 4096, 512], P('section'), may hold values from -0.09375 to 0.09375
- tree_ids: int32 [2, 2048], replicated, may hold values from 0 to 7, as said below
- branch_ids: int32 [2, 2048], replicated, may hold values from 0 to 2, as said below
- span_order: int32 [2, 32], replicated, may hold values from 0 to 31, each once within a row
Outputs:
- layer_out: bfloat16 [8, 2, 2048, 4096], P('section', None, 'seq')
The draws below stay inside these ranges and needn't reach their ends.
Inputs may be any that keep to these rules, and one draw needn't show every extreme that they name: `tree_ids`: in each microbatch nondecreasing along the packed positions, every value of 0 to 7 present, each tree a multiple of 16 positions long. `branch_ids`: within each tree the prompt, chosen and rejected positions come in that order, each branch one position or more. `span_order`: each row is a permutation of 0 to 31.
All inputs are finite; a program needn't handle non-finite values.
Results may differ from the reference program's by a relative error of at most 0.02.
Values may be sent and summed in bfloat16 or wider, within the bound.
No kernel may reach another device: no remote copies, remote signals or barrier semaphores. Data moves between devices by JAX's collectives and lax.ppermute only.
A program may use at most 128 MiB of HBM per device.

```python
import math
import jax
import jax.numpy as jnp
from jax import lax

D = 4096
HQ = 32
HK = 4
HD = 128
MICRO = 2
SEQ_LEN = 2048
TREES = 8
SPAN = 64
SPANS = 32
N_SECTION = 8


def tree_layout(key):
    tree_rows = []
    branch_rows = []
    for microbatch in range(MICRO):
        micro_key = jax.random.fold_in(jax.random.fold_in(key, 7), microbatch)
        key_cuts, key_prompt, key_answer = jax.random.split(micro_key, 3)
        blocks = SEQ_LEN // 16
        candidates = (jax.random.permutation(key_cuts, blocks - 1) + 1).astype(jnp.int32)
        boundary = jnp.sort(candidates[:TREES - 1]) * 16
        positions = jnp.arange(SEQ_LEN, dtype=jnp.int32)
        tree_of = jnp.sum((positions[:, None] >= boundary[None, :]).astype(jnp.int32), axis=1).astype(jnp.int32)
        starts = jnp.concatenate([jnp.zeros((1,), jnp.int32), boundary.astype(jnp.int32)])
        finish = jnp.concatenate([boundary.astype(jnp.int32), jnp.full((1,), SEQ_LEN, jnp.int32)])
        prompt_part = jax.random.randint(key_prompt, (TREES,), 1, 7).astype(jnp.int32)
        answer_part = jax.random.randint(key_answer, (TREES,), 1, 7).astype(jnp.int32)
        cut_one = starts + (finish - starts) * prompt_part // 8
        cut_two = cut_one + jnp.maximum((finish - cut_one) * answer_part // 8, 1)
        branch_of = (positions >= cut_one[tree_of]).astype(jnp.int32) + (positions >= cut_two[tree_of]).astype(jnp.int32)
        tree_rows.append(tree_of)
        branch_rows.append(branch_of)
    return (jnp.stack(tree_rows), jnp.stack(branch_rows))


def draw_tree_ids(key, part):
    return tree_layout(key)[0]


def draw_branch_ids(key, part):
    return tree_layout(key)[1]


def draw_hidden(key, part):
    noise = jax.random.normal(jax.random.fold_in(key, 21), (MICRO, SEQ_LEN, D), jnp.float32)
    values = jnp.clip(noise, -6.0, 6.0)
    return values.astype(jnp.bfloat16)


def draw_key_weight(key, part):
    noise = jnp.clip(jax.random.normal(jax.random.fold_in(key, 22), (N_SECTION, D, HK * HD), jnp.float32), -6.0, 6.0) * D ** (-0.5)
    values = noise
    return values.astype(jnp.bfloat16)


def draw_queries(key, part):
    noise = jnp.clip(jax.random.normal(jax.random.fold_in(key, 23), (N_SECTION, MICRO, SEQ_LEN, HQ * HD), jnp.float32), -6.0, 6.0)
    values = noise
    return values.astype(jnp.bfloat16)


def level_of(stream_key, dims, shards, smallest, high):
    level, own = 1.0, jax.random.fold_in(stream_key, 6)
    for position, shards_of in shards:
        heights = jnp.exp(jax.random.uniform(jax.random.fold_in(own, position), (shards_of,), jnp.float32, smallest / len(shards), high / len(shards)))
        level = level * jnp.repeat(heights, dims[position] // shards_of).reshape([-1 if axis == position else 1 for axis in range(len(dims))])
    return level


def normal_values(own_key, extent, deviation, most, cuts=(), kind=jnp.bfloat16):
    loudness = level_of(own_key, extent, cuts, -0.22, 0.18) if cuts else 1.0
    array = jax.random.normal(own_key, extent, jnp.float32) * deviation * loudness
    return jnp.minimum(jnp.maximum(array, -most), most).astype(kind)


def setup_inputs(seed: int = 0) -> dict:
    key_of = jax.random.split(jax.random.key(seed), 9)
    hidden = draw_hidden(jax.random.fold_in(key_of[8], 71), 0)
    queries = draw_queries(jax.random.fold_in(key_of[8], 71), 0)
    gain = jnp.clip(jnp.exp(math.log(2.0) - 1.3862944 * jax.random.uniform(key_of[2], (N_SECTION, D), jnp.float32) ** level_of(key_of[2], (N_SECTION, D), ((0, 8),), -0.2, 0.2)), 0.5, 2.0)
    key_weight = draw_key_weight(jax.random.fold_in(key_of[8], 71), 0)
    value_weight = normal_values(key_of[4], (N_SECTION, D, HK * HD), D ** -0.5, 0.09375, ((0, 8),))
    tree_ids = draw_tree_ids(jax.random.fold_in(key_of[8], 71), 0)
    branch_ids = draw_branch_ids(jax.random.fold_in(key_of[8], 71), 0)
    span_order = jax.vmap(lambda own: jax.random.permutation(own, SPANS))(jax.random.split(key_of[7], MICRO)).reshape((MICRO, SPANS)).astype(jnp.int32)
    return dict(hidden=hidden, queries=queries, gain=gain, key_weight=key_weight, value_weight=value_weight, tree_ids=tree_ids, branch_ids=branch_ids, span_order=span_order)


rope_base = 500000.0

def frequencies():
    exponent = jnp.arange(HD // 2, dtype=jnp.float32) * (2.0 / HD)
    return jnp.power(jnp.float32(rope_base), -exponent)

def rotate(vectors, angles):
    half_dim = vectors.shape[-1] // 2
    cosine = jnp.cos(angles)[..., None, :]
    sine_part = jnp.sin(angles)[..., None, :]
    lower_half = vectors[..., :half_dim]
    upper_half = vectors[..., half_dim:]
    return jnp.concatenate([lower_half * cosine - upper_half * sine_part, upper_half * cosine + lower_half * sine_part], axis=-1)

def tree_positions(tree_ids, branch_ids):
    positions = jnp.arange(tree_ids.shape[1], dtype=jnp.int32)[None, :]
    opening = jnp.concatenate([jnp.ones_like(tree_ids[:, :1]), (tree_ids[:, 1:] != tree_ids[:, :-1]).astype(jnp.int32)], axis=1)
    starts = lax.cummax(jnp.where(opening > 0, positions, 0).astype(jnp.int32), axis=1)
    chosen = (branch_ids == 1).astype(jnp.int32)
    counted = jnp.cumsum(chosen, axis=1, dtype=jnp.int32)
    before = jnp.take_along_axis(counted - chosen, starts, axis=1)
    skipped = jnp.where(branch_ids == 2, counted - before, 0)
    return (positions - starts - skipped).astype(jnp.int32)

def attend(turned, key_rows, value_rows, allowed):
    ratio = HQ // HK
    scale = 1.0 / math.sqrt(HD)
    grouped = turned.reshape(SEQ_LEN, HK, ratio, HD).transpose(1, 0, 2, 3)

    def one_group(operands):
        query_head, key_head, value_head = operands
        scores = jnp.einsum('qgd,kd->gqk', query_head.astype(jnp.float32), key_head.astype(jnp.float32)) * scale
        masked = jnp.where(allowed[None], scores, -jnp.inf)
        row_top = lax.optimization_barrier(jnp.max(masked, axis=-1, keepdims=True))
        weights = jnp.exp(masked - row_top)
        denominator = lax.optimization_barrier(jnp.sum(weights, axis=-1))
        rounded = lax.optimization_barrier(weights.astype(jnp.bfloat16))
        summed = jnp.einsum('gqk,kd->qgd', rounded.astype(jnp.float32), value_head.astype(jnp.float32))
        return summed / denominator.T[..., None]
    per_head = lax.map(one_group, (grouped, key_rows.transpose(1, 0, 2), value_rows.transpose(1, 0, 2)))
    return per_head.transpose(1, 0, 2, 3).reshape(SEQ_LEN, HQ * HD)

def layer(current, query_rows, gain_row, key_mat, value_mat, rotary_pos, allowed):
    widened = current.astype(jnp.float32)
    norm_scale = lax.rsqrt(lax.optimization_barrier(jnp.mean(widened * widened, axis=-1, keepdims=True)) + 1e-05)
    normed = (widened * norm_scale * gain_row).astype(jnp.bfloat16)
    angles = rotary_pos.astype(jnp.float32)[:, None] * frequencies()
    key_proj = jnp.dot(normed, key_mat, preferred_element_type=jnp.float32).reshape(SEQ_LEN, HK, HD)
    key_rows = rotate(key_proj, angles).astype(jnp.bfloat16)
    value_rows = jnp.dot(normed, value_mat, preferred_element_type=jnp.float32).astype(jnp.bfloat16).reshape(SEQ_LEN, HK, HD)
    turned = rotate(query_rows.astype(jnp.float32).reshape(SEQ_LEN, HQ, HD), angles).astype(jnp.bfloat16)
    attended = attend(turned, key_rows, value_rows, allowed).astype(jnp.bfloat16)
    return (widened + attended.astype(jnp.float32)).astype(jnp.bfloat16)

def reference(hidden, queries, gain, key_weight, value_weight, tree_ids, branch_ids, span_order):
    stored_ids = jnp.arange(SEQ_LEN, dtype=jnp.int32)
    packed_all = jnp.take(span_order, stored_ids // SPAN, axis=1).astype(jnp.int32) * SPAN + stored_ids % SPAN
    rotary_all = tree_positions(tree_ids, branch_ids)
    layers = []
    current = hidden
    for section_id in range(N_SECTION):
        results = []
        for microbatch in range(MICRO):
            packed_rows = packed_all[microbatch]
            tree_of = tree_ids[microbatch][packed_rows]
            branch_of = branch_ids[microbatch][packed_rows]
            rotary_pos = rotary_all[microbatch][packed_rows]
            allowed = (tree_of[:, None] == tree_of[None, :]) & (packed_rows[None, :] <= packed_rows[:, None]) & ((branch_of[None, :] == 0) | (branch_of[None, :] == branch_of[:, None]))
            results.append(layer(current[microbatch], queries[section_id, microbatch], gain[section_id], key_weight[section_id], value_weight[section_id], rotary_pos, allowed))
        current = jnp.stack(results)
        layers.append(current)
    return jnp.stack(layers)
```

```python
import math

import jax
import jax.numpy as jnp
from jax import lax
from jax.experimental import pallas as pl
from jax.experimental.pallas import tpu as pltpu
from jax.sharding import PartitionSpec as P

HQ = 32
HK = 4
HD = 128
SPAN = 64


rope_base = 500000.0


def from_behind(value, axis, by):
    size = lax.axis_size(axis)
    pairs = [(i, i + by) for i in range(size) if 0 <= i + by < size]
    return lax.ppermute(value, axis, pairs)


def frequencies():
    exponent = jnp.arange(HD // 2, dtype=jnp.float32) * (2.0 / HD)
    return jnp.power(jnp.float32(rope_base), -exponent)


def rotate(vectors, cosine, sine_part):
    half_dim = vectors.shape[-1] // 2
    lower_half = vectors[..., :half_dim]
    upper_half = vectors[..., half_dim:]
    return jnp.concatenate(
        [
            lower_half * cosine - upper_half * sine_part,
            upper_half * cosine + lower_half * sine_part,
        ],
        axis=-1,
    )


def tree_positions(tree_ids, branch_ids):
    positions = jnp.arange(tree_ids.shape[1], dtype=jnp.int32)[None, :]
    opening = jnp.concatenate(
        [jnp.ones_like(tree_ids[:, :1]), (tree_ids[:, 1:] != tree_ids[:, :-1]).astype(jnp.int32)],
        axis=1,
    )
    starts = lax.cummax(jnp.where(opening > 0, positions, 0), axis=1)
    chosen = (branch_ids == 1).astype(jnp.int32)
    counted = jnp.cumsum(chosen, axis=1, dtype=jnp.int32)
    before = jnp.take_along_axis(counted - chosen, starts, axis=1)
    skipped = jnp.where(branch_ids == 2, counted - before, 0)
    return positions - starts - skipped


def attention_kernel(q_ref, k_ref, v_ref, bias_ref, res_ref, o_ref):
    ratio = HQ // HK
    scale = 1.0 / math.sqrt(HD)
    keys = k_ref[...]
    values = v_ref[...]
    bias = bias_ref[...]
    for g in range(ratio):
        cols = slice(g * HD, (g + 1) * HD)
        scores = lax.dot_general(
            q_ref[:, cols],
            keys,
            (((1,), (1,)), ((), ())),
            preferred_element_type=jnp.float32,
        )
        masked = scores * scale + bias
        row_top = jnp.max(masked, axis=-1, keepdims=True)
        weights = jnp.exp(masked - row_top)
        denominator = jnp.sum(weights, axis=-1, keepdims=True)
        summed = jnp.dot(
            weights.astype(jnp.bfloat16), values, preferred_element_type=jnp.float32
        )
        attended = (summed / denominator).astype(jnp.bfloat16)
        o_ref[:, cols] = (
            res_ref[:, cols].astype(jnp.float32) + attended.astype(jnp.float32)
        ).astype(o_ref.dtype)


def attention(turned, kv_all, bias, residual):
    rows, width = turned.shape
    keys_len = kv_all.shape[0]
    group = width // HK
    return pl.pallas_call(
        attention_kernel,
        grid=(HK,),
        in_specs=[
            pl.BlockSpec((rows, group), lambda k: (0, k)),
            pl.BlockSpec((keys_len, HD), lambda k: (0, k)),
            pl.BlockSpec((keys_len, HD), lambda k: (0, HK + k)),
            pl.BlockSpec((rows, keys_len), lambda k: (0, 0)),
            pl.BlockSpec((rows, group), lambda k: (0, k)),
        ],
        out_specs=pl.BlockSpec((rows, group), lambda k: (0, k)),
        out_shape=jax.ShapeDtypeStruct((rows, width), jnp.bfloat16),
    )(turned, kv_all, kv_all, bias, residual)


def local(hidden, queries, gain, key_weight, value_weight, tree_ids, branch_ids, span_order):
    section_id = lax.axis_index("section")
    shard_id = lax.axis_index("seq")
    section_count = lax.axis_size("section")
    micro_count, row_count, model_width = hidden.shape
    seq_len = tree_ids.shape[1]
    rotary_all = tree_positions(tree_ids, branch_ids)
    stored_ids = jnp.arange(seq_len, dtype=jnp.int32)
    packed_all = jnp.take(span_order, stored_ids // SPAN, axis=1) * SPAN + stored_ids % SPAN
    key_tree = jnp.take_along_axis(tree_ids, packed_all, axis=1)
    key_branch = jnp.take_along_axis(branch_ids, packed_all, axis=1)
    key_rotary = jnp.take_along_axis(rotary_all, packed_all, axis=1)
    first_row = shard_id * row_count
    own_packed = lax.dynamic_slice_in_dim(packed_all, first_row, row_count, 1)
    own_tree = lax.dynamic_slice_in_dim(key_tree, first_row, row_count, 1)
    own_branch = lax.dynamic_slice_in_dim(key_branch, first_row, row_count, 1)
    own_rotary = lax.dynamic_slice_in_dim(key_rotary, first_row, row_count, 1)
    allowed = (
        (own_tree[:, :, None] == key_tree[:, None, :])
        & (packed_all[:, None, :] <= own_packed[:, :, None])
        & ((key_branch[:, None, :] == 0) | (key_branch[:, None, :] == own_branch[:, :, None]))
    )
    bias_all = jnp.where(allowed, 0.0, -jnp.inf).astype(jnp.float32)
    angles = own_rotary.astype(jnp.float32)[..., None] * frequencies()
    cos_all = jnp.cos(angles)
    sin_all = jnp.sin(angles)
    gain_row = gain[0]
    key_mat = key_weight[0]
    value_mat = value_weight[0]
    kv_mat = jnp.concatenate([key_mat, value_mat], axis=1)

    def run_layer(current, mb):
        cosine = lax.dynamic_index_in_dim(cos_all, mb, 0, keepdims=False)
        sine_part = lax.dynamic_index_in_dim(sin_all, mb, 0, keepdims=False)
        bias = lax.dynamic_index_in_dim(bias_all, mb, 0, keepdims=False)
        widened = current.astype(jnp.float32)
        norm_scale = lax.rsqrt(jnp.mean(widened * widened, axis=-1, keepdims=True) + 1e-05)
        normed = (widened * norm_scale * gain_row).astype(jnp.bfloat16)
        kv_proj = jnp.dot(normed, kv_mat, preferred_element_type=jnp.float32)
        key_proj = kv_proj[:, : HK * HD].reshape(row_count, HK, HD)
        key_rows = (
            rotate(key_proj, cosine[:, None, :], sine_part[:, None, :])
            .astype(jnp.bfloat16)
            .reshape(row_count, HK * HD)
        )
        value_rows = kv_proj[:, HK * HD :].astype(jnp.bfloat16)
        kv_rows = jnp.concatenate([key_rows, value_rows], axis=1)
        kv_all = lax.all_gather(kv_rows, "seq", axis=0, tiled=True)
        query_local = lax.dynamic_index_in_dim(queries[0], mb, 0, keepdims=False)
        turned = (
            rotate(
                query_local.astype(jnp.float32).reshape(row_count, HQ, HD),
                cosine[:, None, :],
                sine_part[:, None, :],
            )
            .astype(jnp.bfloat16)
            .reshape(row_count, HQ * HD)
        )
        return attention(turned, kv_all, bias, current)

    tick_count = section_count + micro_count - 1

    def advance(step_id, state_pair):
        previous, outputs = state_pair
        incoming = from_behind(previous, "section", 1)
        first_mb = step_id - section_id
        active = (first_mb >= 0) & (first_mb < micro_count)
        start_at = jnp.clip(first_mb, 0, micro_count - 1)
        entering = lax.dynamic_index_in_dim(hidden, start_at, 0, keepdims=False)
        current = jnp.where(section_id == 0, entering, incoming)
        computed = run_layer(current, start_at)
        result = jnp.where(active, computed, jnp.zeros_like(computed))
        stored = lax.dynamic_update_index_in_dim(outputs, result, start_at, 0)
        outputs = jnp.where(active, stored, outputs)
        return (result, outputs)

    empty_pass = jnp.zeros((row_count, model_width), jnp.bfloat16)
    empty_out = jnp.zeros((micro_count, row_count, model_width), jnp.bfloat16)
    final_pass, outputs = lax.fori_loop(0, tick_count, advance, (empty_pass, empty_out))
    return outputs[None]


def solution(mesh):
    placed = (
        P(None, "seq", None),
        P("section", None, "seq", None),
        P("section", None),
        P("section", None, None),
        P("section", None, None),
        P(),
        P(),
        P(),
    )
    return jax.shard_map(
        local,
        mesh=mesh,
        in_specs=placed,
        out_specs=P("section", None, "seq", None),
        check_vma=False,
    )
```

```python
import math

import jax
import jax.numpy as jnp
from jax import lax
from jax.experimental import pallas as pl
from jax.experimental.pallas import tpu as pltpu
from jax.sharding import PartitionSpec as P

HQ = 32
HK = 4
HD = 128
SPAN = 64


rope_base = 500000.0


def from_behind(value, axis, by):
    size = lax.axis_size(axis)
    pairs = [(i, i + by) for i in range(size) if 0 <= i + by < size]
    return lax.ppermute(value, axis, pairs)


def frequencies():
    exponent = jnp.arange(HD // 2, dtype=jnp.float32) * (2.0 / HD)
    return jnp.power(jnp.float32(rope_base), -exponent)


def rotate(vectors, cosine, sine_part):
    half_dim = vectors.shape[-1] // 2
    lower_half = vectors[..., :half_dim]
    upper_half = vectors[..., half_dim:]
    return jnp.concatenate(
        [
            lower_half * cosine - upper_half * sine_part,
            upper_half * cosine + lower_half * sine_part,
        ],
        axis=-1,
    )


def tree_positions(tree_ids, branch_ids):
    trees = jnp.arange(8, dtype=jnp.int32)[None, :, None]
    positions = jnp.arange(tree_ids.shape[1], dtype=jnp.int32)[None, :]
    same = tree_ids[:, None, :] == trees
    starts = jnp.sum((tree_ids[:, None, :] < trees).astype(jnp.int32), axis=2)
    chosen = jnp.sum((same & (branch_ids[:, None, :] == 1)).astype(jnp.int32), axis=2)
    own_start = jnp.sum(jnp.where(same, starts[:, :, None], 0), axis=1)
    own_chosen = jnp.sum(jnp.where(same, chosen[:, :, None], 0), axis=1)
    skipped = jnp.where(branch_ids == 2, own_chosen, 0)
    return positions - own_start - skipped


def by_span(values, span_order):
    micro_count, seq_len = values.shape
    spans = seq_len // SPAN
    blocks = values.reshape(micro_count, 1, spans, SPAN)
    picks = span_order[:, :, None] == jnp.arange(spans, dtype=jnp.int32)[None, None, :]
    chosen = jnp.where(picks[..., None], blocks, 0)
    return jnp.sum(chosen, axis=2).reshape(micro_count, seq_len)


def attention_kernel(q_ref, k_ref, v_ref, bias_ref, res_ref, o_ref):
    ratio = HQ // HK
    scale = 1.0 / math.sqrt(HD)
    keys = k_ref[...]
    values = v_ref[...]
    bias = bias_ref[...]
    for g in range(ratio):
        cols = slice(g * HD, (g + 1) * HD)
        scores = lax.dot_general(
            q_ref[:, cols],
            keys,
            (((1,), (1,)), ((), ())),
            preferred_element_type=jnp.float32,
        )
        masked = scores * scale + bias
        row_top = jnp.max(masked, axis=-1, keepdims=True)
        weights = jnp.exp(masked - row_top)
        denominator = jnp.sum(weights, axis=-1, keepdims=True)
        summed = jnp.dot(
            weights.astype(jnp.bfloat16), values, preferred_element_type=jnp.float32
        )
        attended = (summed / denominator).astype(jnp.bfloat16)
        o_ref[:, cols] = (
            res_ref[:, cols].astype(jnp.float32) + attended.astype(jnp.float32)
        ).astype(o_ref.dtype)


def attention(turned, kv_all, bias, residual):
    rows, width = turned.shape
    keys_len = kv_all.shape[0]
    group = width // HK
    return pl.pallas_call(
        attention_kernel,
        grid=(HK,),
        in_specs=[
            pl.BlockSpec((rows, group), lambda k: (0, k)),
            pl.BlockSpec((keys_len, HD), lambda k: (0, k)),
            pl.BlockSpec((keys_len, HD), lambda k: (0, HK + k)),
            pl.BlockSpec((rows, keys_len), lambda k: (0, 0)),
            pl.BlockSpec((rows, group), lambda k: (0, k)),
        ],
        out_specs=pl.BlockSpec((rows, group), lambda k: (0, k)),
        out_shape=jax.ShapeDtypeStruct((rows, width), jnp.bfloat16),
    )(turned, kv_all, kv_all, bias, residual)


def local(hidden, queries, gain, key_weight, value_weight, tree_ids, branch_ids, span_order):
    section_id = lax.axis_index("section")
    shard_id = lax.axis_index("seq")
    section_count = lax.axis_size("section")
    micro_count, row_count, model_width = hidden.shape
    seq_len = tree_ids.shape[1]
    rotary_all = tree_positions(tree_ids, branch_ids)
    stored_ids = jnp.arange(seq_len, dtype=jnp.int32)
    packed_all = jnp.repeat(span_order, SPAN, axis=1) * SPAN + stored_ids % SPAN
    key_tree = by_span(tree_ids, span_order)
    key_branch = by_span(branch_ids, span_order)
    key_rotary = by_span(rotary_all, span_order)
    first_row = shard_id * row_count
    own_packed = lax.dynamic_slice_in_dim(packed_all, first_row, row_count, 1)
    own_tree = lax.dynamic_slice_in_dim(key_tree, first_row, row_count, 1)
    own_branch = lax.dynamic_slice_in_dim(key_branch, first_row, row_count, 1)
    own_rotary = lax.dynamic_slice_in_dim(key_rotary, first_row, row_count, 1)
    allowed = (
        (own_tree[:, :, None] == key_tree[:, None, :])
        & (packed_all[:, None, :] <= own_packed[:, :, None])
        & ((key_branch[:, None, :] == 0) | (key_branch[:, None, :] == own_branch[:, :, None]))
    )
    bias_all = jnp.where(allowed, 0.0, -jnp.inf).astype(jnp.float32)
    angles = own_rotary.astype(jnp.float32)[..., None] * frequencies()
    cos_all = jnp.cos(angles)
    sin_all = jnp.sin(angles)
    gain_row = gain[0]
    key_mat = key_weight[0]
    value_mat = value_weight[0]
    kv_mat = jnp.concatenate([key_mat, value_mat], axis=1)

    def run_layer(current, mb):
        cosine = lax.dynamic_index_in_dim(cos_all, mb, 0, keepdims=False)
        sine_part = lax.dynamic_index_in_dim(sin_all, mb, 0, keepdims=False)
        bias = lax.dynamic_index_in_dim(bias_all, mb, 0, keepdims=False)
        widened = current.astype(jnp.float32)
        norm_scale = lax.rsqrt(jnp.mean(widened * widened, axis=-1, keepdims=True) + 1e-05)
        normed = (widened * norm_scale * gain_row).astype(jnp.bfloat16)
        kv_proj = jnp.dot(normed, kv_mat, preferred_element_type=jnp.float32)
        key_proj = kv_proj[:, : HK * HD].reshape(row_count, HK, HD)
        key_rows = (
            rotate(key_proj, cosine[:, None, :], sine_part[:, None, :])
            .astype(jnp.bfloat16)
            .reshape(row_count, HK * HD)
        )
        value_rows = kv_proj[:, HK * HD :].astype(jnp.bfloat16)
        kv_rows = jnp.concatenate([key_rows, value_rows], axis=1)
        kv_all = lax.all_gather(kv_rows, "seq", axis=0, tiled=True)
        query_local = lax.dynamic_index_in_dim(queries[0], mb, 0, keepdims=False)
        turned = (
            rotate(
                query_local.astype(jnp.float32).reshape(row_count, HQ, HD),
                cosine[:, None, :],
                sine_part[:, None, :],
            )
            .astype(jnp.bfloat16)
            .reshape(row_count, HQ * HD)
        )
        return attention(turned, kv_all, bias, current)

    tick_count = section_count + micro_count - 1

    def advance(step_id, state_pair):
        previous, outputs = state_pair
        incoming = from_behind(previous, "section", 1)
        first_mb = step_id - section_id
        active = (first_mb >= 0) & (first_mb < micro_count)
        start_at = jnp.clip(first_mb, 0, micro_count - 1)
        entering = lax.dynamic_index_in_dim(hidden, start_at, 0, keepdims=False)
        current = jnp.where(section_id == 0, entering, incoming)
        computed = run_layer(current, start_at)
        result = jnp.where(active, computed, jnp.zeros_like(computed))
        stored = lax.dynamic_update_index_in_dim(outputs, result, start_at, 0)
        outputs = jnp.where(active, stored, outputs)
        return (result, outputs)

    empty_pass = jnp.zeros((row_count, model_width), jnp.bfloat16)
    empty_out = jnp.zeros((micro_count, row_count, model_width), jnp.bfloat16)
    final_pass, outputs = lax.fori_loop(0, tick_count, advance, (empty_pass, empty_out))
    return outputs[None]


def solution(mesh):
    placed = (
        P(None, "seq", None),
        P("section", None, "seq", None),
        P("section", None),
        P("section", None, None),
        P("section", None, None),
        P(),
        P(),
        P(),
    )
    return jax.shard_map(
        local,
        mesh=mesh,
        in_specs=placed,
        out_specs=P("section", None, "seq", None),
        check_vma=False,
    )
```

```python
import math

import jax
import jax.numpy as jnp
from jax import lax
from jax.experimental import pallas as pl
from jax.experimental.pallas import tpu as pltpu
from jax.sharding import PartitionSpec as P

HQ = 32
HK = 4
HD = 128
SPAN = 64


rope_base = 500000.0


def from_behind(value, axis, by):
    size = lax.axis_size(axis)
    pairs = [(i, i + by) for i in range(size) if 0 <= i + by < size]
    return lax.ppermute(value, axis, pairs)


def frequencies():
    exponent = jnp.arange(HD // 2, dtype=jnp.float32) * (2.0 / HD)
    return jnp.power(jnp.float32(rope_base), -exponent)


def rotate(vectors, cosine, sine_part):
    half_dim = vectors.shape[-1] // 2
    lower_half = vectors[..., :half_dim]
    upper_half = vectors[..., half_dim:]
    return jnp.concatenate(
        [
            lower_half * cosine - upper_half * sine_part,
            upper_half * cosine + lower_half * sine_part,
        ],
        axis=-1,
    )


def tree_positions(tree_ids, branch_ids):
    trees = jnp.arange(8, dtype=jnp.int32)[None, :, None]
    positions = jnp.arange(tree_ids.shape[1], dtype=jnp.int32)[None, :]
    same = tree_ids[:, None, :] == trees
    starts = jnp.sum((tree_ids[:, None, :] < trees).astype(jnp.int32), axis=2)
    chosen = jnp.sum((same & (branch_ids[:, None, :] == 1)).astype(jnp.int32), axis=2)
    own_start = jnp.sum(jnp.where(same, starts[:, :, None], 0), axis=1)
    own_chosen = jnp.sum(jnp.where(same, chosen[:, :, None], 0), axis=1)
    skipped = jnp.where(branch_ids == 2, own_chosen, 0)
    return positions - own_start - skipped


def by_span(values, span_order):
    micro_count, seq_len = values.shape
    spans = seq_len // SPAN
    blocks = values.reshape(micro_count, 1, spans, SPAN)
    picks = span_order[:, :, None] == jnp.arange(spans, dtype=jnp.int32)[None, None, :]
    chosen = jnp.where(picks[..., None], blocks, 0)
    return jnp.sum(chosen, axis=2).reshape(micro_count, seq_len)


def attention_kernel(q_ref, k_ref, v_ref, bias_ref, res_ref, *rest):
    o_ref = rest[-1]
    ratio = HQ // HK
    scale = 1.0 / math.sqrt(HD)
    keys = k_ref[...]
    values = v_ref[...]
    bias = bias_ref[...]
    for g in range(ratio):
        cols = slice(g * HD, (g + 1) * HD)
        scores = lax.dot_general(
            q_ref[:, cols],
            keys,
            (((1,), (1,)), ((), ())),
            preferred_element_type=jnp.float32,
        )
        masked = scores * scale + bias
        row_top = jnp.max(masked, axis=-1, keepdims=True)
        weights = jnp.exp(masked - row_top)
        denominator = jnp.sum(weights, axis=-1, keepdims=True)
        summed = jnp.dot(
            weights.astype(jnp.bfloat16), values, preferred_element_type=jnp.float32
        )
        attended = (summed / denominator).astype(jnp.bfloat16)
        o_ref[:, cols] = (
            res_ref[:, cols].astype(jnp.float32) + attended.astype(jnp.float32)
        ).astype(o_ref.dtype)


def attention(turned, kv_part, bias, residual, first, base=None):
    rows, width = turned.shape
    keys_len = kv_part.shape[0]
    group = width // HK
    heads = kv_part.shape[1] // (2 * HD)
    in_specs = [
        pl.BlockSpec((rows, group), lambda k: (0, first + k)),
        pl.BlockSpec((keys_len, HD), lambda k: (0, k)),
        pl.BlockSpec((keys_len, HD), lambda k: (0, heads + k)),
        pl.BlockSpec((rows, keys_len), lambda k: (0, 0)),
        pl.BlockSpec((rows, group), lambda k: (0, first + k)),
    ]
    operands = [turned, kv_part, kv_part, bias, residual]
    aliases = {}
    if base is not None:
        in_specs.append(pl.BlockSpec(memory_space=pl.ANY))
        operands.append(base)
        aliases = {len(operands) - 1: 0}
    return pl.pallas_call(
        attention_kernel,
        grid=(heads,),
        in_specs=in_specs,
        out_specs=pl.BlockSpec((rows, group), lambda k: (0, first + k)),
        out_shape=jax.ShapeDtypeStruct((rows, width), jnp.bfloat16),
        input_output_aliases=aliases,
    )(*operands)


def local(hidden, queries, gain, key_weight, value_weight, tree_ids, branch_ids, span_order):
    section_id = lax.axis_index("section")
    shard_id = lax.axis_index("seq")
    section_count = lax.axis_size("section")
    micro_count, row_count, model_width = hidden.shape
    seq_len = tree_ids.shape[1]
    rotary_all = tree_positions(tree_ids, branch_ids)
    stored_ids = jnp.arange(seq_len, dtype=jnp.int32)
    packed_all = jnp.repeat(span_order, SPAN, axis=1) * SPAN + stored_ids % SPAN
    key_tree = by_span(tree_ids, span_order)
    key_branch = by_span(branch_ids, span_order)
    key_rotary = by_span(rotary_all, span_order)
    first_row = shard_id * row_count
    own_packed = lax.dynamic_slice_in_dim(packed_all, first_row, row_count, 1)
    own_tree = lax.dynamic_slice_in_dim(key_tree, first_row, row_count, 1)
    own_branch = lax.dynamic_slice_in_dim(key_branch, first_row, row_count, 1)
    own_rotary = lax.dynamic_slice_in_dim(key_rotary, first_row, row_count, 1)
    allowed = (
        (own_tree[:, :, None] == key_tree[:, None, :])
        & (packed_all[:, None, :] <= own_packed[:, :, None])
        & ((key_branch[:, None, :] == 0) | (key_branch[:, None, :] == own_branch[:, :, None]))
    )
    bias_all = jnp.where(allowed, 0.0, -jnp.inf).astype(jnp.float32)
    angles = own_rotary.astype(jnp.float32)[..., None] * frequencies()
    cos_all = jnp.cos(angles)
    sin_all = jnp.sin(angles)
    gain_row = gain[0]
    key_mat = key_weight[0]
    value_mat = value_weight[0]
    kv_mat = jnp.concatenate([key_mat, value_mat], axis=1)

    def run_layer(current, mb):
        cosine = lax.dynamic_index_in_dim(cos_all, mb, 0, keepdims=False)
        sine_part = lax.dynamic_index_in_dim(sin_all, mb, 0, keepdims=False)
        bias = lax.dynamic_index_in_dim(bias_all, mb, 0, keepdims=False)
        widened = current.astype(jnp.float32)
        norm_scale = lax.rsqrt(jnp.mean(widened * widened, axis=-1, keepdims=True) + 1e-05)
        normed = (widened * norm_scale * gain_row).astype(jnp.bfloat16)
        kv_proj = jnp.dot(normed, kv_mat, preferred_element_type=jnp.float32)
        key_proj = kv_proj[:, : HK * HD].reshape(row_count, HK, HD)
        key_rows = (
            rotate(key_proj, cosine[:, None, :], sine_part[:, None, :])
            .astype(jnp.bfloat16)
            .reshape(row_count, HK * HD)
        )
        value_rows = kv_proj[:, HK * HD :].astype(jnp.bfloat16)
        half = HK // 2 * HD
        kv_front = jnp.concatenate([key_rows[:, :half], value_rows[:, :half]], axis=1)
        kv_back = jnp.concatenate([key_rows[:, half:], value_rows[:, half:]], axis=1)
        front_all = lax.all_gather(kv_front, "seq", axis=0, tiled=True)
        back_all = lax.all_gather(kv_back, "seq", axis=0, tiled=True)
        query_local = lax.dynamic_index_in_dim(queries[0], mb, 0, keepdims=False)
        turned = (
            rotate(
                query_local.astype(jnp.float32).reshape(row_count, HQ, HD),
                cosine[:, None, :],
                sine_part[:, None, :],
            )
            .astype(jnp.bfloat16)
            .reshape(row_count, HQ * HD)
        )
        partial = attention(turned, front_all, bias, current, 0)
        return attention(turned, back_all, bias, current, HK // 2, partial)

    tick_count = section_count + micro_count - 1

    def advance(step_id, state_pair):
        previous, outputs = state_pair
        incoming = from_behind(previous, "section", 1)
        first_mb = step_id - section_id
        active = (first_mb >= 0) & (first_mb < micro_count)
        start_at = jnp.clip(first_mb, 0, micro_count - 1)
        entering = lax.dynamic_index_in_dim(hidden, start_at, 0, keepdims=False)
        current = jnp.where(section_id == 0, entering, incoming)
        computed = run_layer(current, start_at)
        result = jnp.where(active, computed, jnp.zeros_like(computed))
        stored = lax.dynamic_update_index_in_dim(outputs, result, start_at, 0)
        outputs = jnp.where(active, stored, outputs)
        return (result, outputs)

    empty_pass = jnp.zeros((row_count, model_width), jnp.bfloat16)
    empty_out = jnp.zeros((micro_count, row_count, model_width), jnp.bfloat16)
    final_pass, outputs = lax.fori_loop(0, tick_count, advance, (empty_pass, empty_out))
    return outputs[None]


def solution(mesh):
    placed = (
        P(None, "seq", None),
        P("section", None, "seq", None),
        P("section", None),
        P("section", None, None),
        P("section", None, None),
        P(),
        P(),
        P(),
    )
    return jax.shard_map(
        local,
        mesh=mesh,
        in_specs=placed,
        out_specs=P("section", None, "seq", None),
        check_vma=False,
    )
```

```python
import math

import jax
import jax.numpy as jnp
from jax import lax
from jax.experimental import pallas as pl
from jax.experimental.pallas import tpu as pltpu
from jax.sharding import PartitionSpec as P

HQ = 32
HK = 4
HD = 128
SPAN = 64


rope_base = 500000.0


def from_behind(value, axis, by):
    size = lax.axis_size(axis)
    pairs = [(i, i + by) for i in range(size) if 0 <= i + by < size]
    return lax.ppermute(value, axis, pairs)


def frequencies():
    exponent = jnp.arange(HD // 2, dtype=jnp.float32) * (2.0 / HD)
    return jnp.power(jnp.float32(rope_base), -exponent)


def rotate(vectors, cosine, sine_part):
    half_dim = vectors.shape[-1] // 2
    lower_half = vectors[..., :half_dim]
    upper_half = vectors[..., half_dim:]
    return jnp.concatenate(
        [
            lower_half * cosine - upper_half * sine_part,
            upper_half * cosine + lower_half * sine_part,
        ],
        axis=-1,
    )


def tree_positions(tree_ids, branch_ids):
    trees = jnp.arange(8, dtype=jnp.int32)[None, :, None]
    positions = jnp.arange(tree_ids.shape[1], dtype=jnp.int32)[None, :]
    same = tree_ids[:, None, :] == trees
    starts = jnp.sum((tree_ids[:, None, :] < trees).astype(jnp.int32), axis=2)
    chosen = jnp.sum((same & (branch_ids[:, None, :] == 1)).astype(jnp.int32), axis=2)
    own_start = jnp.sum(jnp.where(same, starts[:, :, None], 0), axis=1)
    own_chosen = jnp.sum(jnp.where(same, chosen[:, :, None], 0), axis=1)
    skipped = jnp.where(branch_ids == 2, own_chosen, 0)
    return positions - own_start - skipped


def by_span(values, span_order):
    micro_count, seq_len = values.shape
    spans = seq_len // SPAN
    blocks = values.reshape(micro_count, 1, spans, SPAN)
    picks = span_order[:, :, None] == jnp.arange(spans, dtype=jnp.int32)[None, None, :]
    chosen = jnp.where(picks[..., None], blocks, 0)
    return jnp.sum(chosen, axis=2).reshape(micro_count, seq_len)


def ring_gather(value, shift):
    ahead = shift(value, 1)
    behind = shift(value, -1)
    width = value.shape[1] // 2
    far = jnp.concatenate(
        [shift(ahead[:, :width], 1), shift(behind[:, width:], -1)], axis=1
    )
    return [value, ahead, behind, far]


RING_OFFSETS = (0, -1, 1, 2)


def torus_gather(value, side):
    def shifter(along_z):
        def shift(piece, by):
            pairs = []
            for z in range(side):
                for x in range(side):
                    if along_z:
                        pairs.append((z * side + x, ((z + by) % side) * side + x))
                    else:
                        pairs.append((z * side + x, z * side + (x + by) % side))
            return lax.ppermute(piece, "seq", pairs)

        return shift

    shift_z = shifter(True)
    shift_x = shifter(False)
    rows = value.shape[0]
    width = value.shape[1] // 2
    row_a = jnp.concatenate(ring_gather(value[:, :width], shift_x), axis=0)
    full_a = jnp.concatenate(ring_gather(row_a, shift_z), axis=0)
    col_b = jnp.concatenate(ring_gather(value[:, width:], shift_z), axis=0)
    pieces_b = ring_gather(col_b, shift_x)
    full_b = jnp.stack(pieces_b, axis=0).reshape(side, side, rows, width)
    full_b = full_b.transpose(1, 0, 2, 3).reshape(side * side * rows, width)
    return jnp.concatenate([full_a, full_b], axis=1)


def torus_order(values, shard_id, side, rows):
    micro_count = values.shape[0]
    z = shard_id // side
    x = shard_id % side
    blocks = values.reshape(micro_count, side, side, rows)
    blocks = jnp.roll(blocks, -z, axis=1)
    blocks = jnp.roll(blocks, -x, axis=2)
    picks = [o % side for o in RING_OFFSETS]
    blocks = jnp.stack([blocks[:, p] for p in picks], axis=1)
    blocks = jnp.stack([blocks[:, :, q] for q in picks], axis=2)
    return blocks.reshape(micro_count, side * side * rows)


def attention_kernel(q_ref, k_ref, v_ref, bias_ref, res_ref, o_ref):
    ratio = HQ // HK
    scale = 1.0 / math.sqrt(HD)
    keys = k_ref[...]
    values = v_ref[...]
    bias = bias_ref[...]
    for g in range(ratio):
        cols = slice(g * HD, (g + 1) * HD)
        scores = lax.dot_general(
            q_ref[:, cols],
            keys,
            (((1,), (1,)), ((), ())),
            preferred_element_type=jnp.float32,
        )
        masked = scores * scale + bias
        row_top = jnp.max(masked, axis=-1, keepdims=True)
        weights = jnp.exp(masked - row_top)
        denominator = jnp.sum(weights, axis=-1, keepdims=True)
        summed = jnp.dot(
            weights.astype(jnp.bfloat16), values, preferred_element_type=jnp.float32
        )
        attended = (summed / denominator).astype(jnp.bfloat16)
        o_ref[:, cols] = (
            res_ref[:, cols].astype(jnp.float32) + attended.astype(jnp.float32)
        ).astype(o_ref.dtype)


def attention(turned, kv_all, bias, residual):
    rows, width = turned.shape
    keys_len = kv_all.shape[0]
    group = width // HK
    return pl.pallas_call(
        attention_kernel,
        grid=(HK,),
        in_specs=[
            pl.BlockSpec((rows, group), lambda k: (0, k)),
            pl.BlockSpec((keys_len, HD), lambda k: (0, k)),
            pl.BlockSpec((keys_len, HD), lambda k: (0, HK + k)),
            pl.BlockSpec((rows, keys_len), lambda k: (0, 0)),
            pl.BlockSpec((rows, group), lambda k: (0, k)),
        ],
        out_specs=pl.BlockSpec((rows, group), lambda k: (0, k)),
        out_shape=jax.ShapeDtypeStruct((rows, width), jnp.bfloat16),
    )(turned, kv_all, kv_all, bias, residual)


def local(hidden, queries, gain, key_weight, value_weight, tree_ids, branch_ids, span_order):
    section_id = lax.axis_index("section")
    shard_id = lax.axis_index("seq")
    section_count = lax.axis_size("section")
    micro_count, row_count, model_width = hidden.shape
    seq_len = tree_ids.shape[1]
    rotary_all = tree_positions(tree_ids, branch_ids)
    stored_ids = jnp.arange(seq_len, dtype=jnp.int32)
    packed_all = jnp.repeat(span_order, SPAN, axis=1) * SPAN + stored_ids % SPAN
    key_tree = by_span(tree_ids, span_order)
    key_branch = by_span(branch_ids, span_order)
    key_rotary = by_span(rotary_all, span_order)
    first_row = shard_id * row_count
    own_packed = lax.dynamic_slice_in_dim(packed_all, first_row, row_count, 1)
    own_tree = lax.dynamic_slice_in_dim(key_tree, first_row, row_count, 1)
    own_branch = lax.dynamic_slice_in_dim(key_branch, first_row, row_count, 1)
    own_rotary = lax.dynamic_slice_in_dim(key_rotary, first_row, row_count, 1)
    seq_count = lax.axis_size("seq")
    side = math.isqrt(seq_count)
    order_tree = torus_order(key_tree, shard_id, side, row_count)
    order_branch = torus_order(key_branch, shard_id, side, row_count)
    order_packed = torus_order(packed_all, shard_id, side, row_count)
    allowed = (
        (own_tree[:, :, None] == order_tree[:, None, :])
        & (order_packed[:, None, :] <= own_packed[:, :, None])
        & ((order_branch[:, None, :] == 0) | (order_branch[:, None, :] == own_branch[:, :, None]))
    )
    bias_all = jnp.where(allowed, 0.0, -jnp.inf).astype(jnp.float32)
    angles = own_rotary.astype(jnp.float32)[..., None] * frequencies()
    cos_all = jnp.cos(angles)
    sin_all = jnp.sin(angles)
    gain_row = gain[0]
    key_mat = key_weight[0]
    value_mat = value_weight[0]
    kv_mat = jnp.concatenate([key_mat, value_mat], axis=1)

    def run_layer(current, mb):
        cosine = lax.dynamic_index_in_dim(cos_all, mb, 0, keepdims=False)
        sine_part = lax.dynamic_index_in_dim(sin_all, mb, 0, keepdims=False)
        bias = lax.dynamic_index_in_dim(bias_all, mb, 0, keepdims=False)
        widened = current.astype(jnp.float32)
        norm_scale = lax.rsqrt(jnp.mean(widened * widened, axis=-1, keepdims=True) + 1e-05)
        normed = (widened * norm_scale * gain_row).astype(jnp.bfloat16)
        kv_proj = jnp.dot(normed, kv_mat, preferred_element_type=jnp.float32)
        key_proj = kv_proj[:, : HK * HD].reshape(row_count, HK, HD)
        key_rows = (
            rotate(key_proj, cosine[:, None, :], sine_part[:, None, :])
            .astype(jnp.bfloat16)
            .reshape(row_count, HK * HD)
        )
        value_rows = kv_proj[:, HK * HD :].astype(jnp.bfloat16)
        kv_rows = jnp.concatenate([key_rows, value_rows], axis=1)
        kv_all = torus_gather(kv_rows, side)
        query_local = lax.dynamic_index_in_dim(queries[0], mb, 0, keepdims=False)
        turned = (
            rotate(
                query_local.astype(jnp.float32).reshape(row_count, HQ, HD),
                cosine[:, None, :],
                sine_part[:, None, :],
            )
            .astype(jnp.bfloat16)
            .reshape(row_count, HQ * HD)
        )
        return attention(turned, kv_all, bias, current)

    tick_count = section_count + micro_count - 1

    def advance(step_id, state_pair):
        previous, outputs = state_pair
        incoming = from_behind(previous, "section", 1)
        first_mb = step_id - section_id
        active = (first_mb >= 0) & (first_mb < micro_count)
        start_at = jnp.clip(first_mb, 0, micro_count - 1)
        entering = lax.dynamic_index_in_dim(hidden, start_at, 0, keepdims=False)
        current = jnp.where(section_id == 0, entering, incoming)
        computed = run_layer(current, start_at)
        result = jnp.where(active, computed, jnp.zeros_like(computed))
        stored = lax.dynamic_update_index_in_dim(outputs, result, start_at, 0)
        outputs = jnp.where(active, stored, outputs)
        return (result, outputs)

    empty_pass = jnp.zeros((row_count, model_width), jnp.bfloat16)
    empty_out = jnp.zeros((micro_count, row_count, model_width), jnp.bfloat16)
    final_pass, outputs = lax.fori_loop(0, tick_count, advance, (empty_pass, empty_out))
    return outputs[None]


def solution(mesh):
    placed = (
        P(None, "seq", None),
        P("section", None, "seq", None),
        P("section", None),
        P("section", None, None),
        P("section", None, None),
        P(),
        P(),
        P(),
    )
    return jax.shard_map(
        local,
        mesh=mesh,
        in_specs=placed,
        out_specs=P("section", None, "seq", None),
        check_vma=False,
    )
```

```python
import math

import jax
import jax.numpy as jnp
from jax import lax
from jax.experimental import pallas as pl
from jax.experimental.pallas import tpu as pltpu
from jax.sharding import PartitionSpec as P

HQ = 32
HK = 4
HD = 128
SPAN = 64


rope_base = 500000.0


def from_behind(value, axis, by):
    size = lax.axis_size(axis)
    pairs = [(i, i + by) for i in range(size) if 0 <= i + by < size]
    return lax.ppermute(value, axis, pairs)


def frequencies():
    exponent = jnp.arange(HD // 2, dtype=jnp.float32) * (2.0 / HD)
    return jnp.power(jnp.float32(rope_base), -exponent)


def rotate(vectors, cosine, sine_part):
    half_dim = vectors.shape[-1] // 2
    lower_half = vectors[..., :half_dim]
    upper_half = vectors[..., half_dim:]
    return jnp.concatenate(
        [
            lower_half * cosine - upper_half * sine_part,
            upper_half * cosine + lower_half * sine_part,
        ],
        axis=-1,
    )


def tree_positions(tree_ids, branch_ids):
    trees = jnp.arange(8, dtype=jnp.int32)[None, :, None]
    positions = jnp.arange(tree_ids.shape[1], dtype=jnp.int32)[None, :]
    same = tree_ids[:, None, :] == trees
    starts = jnp.sum((tree_ids[:, None, :] < trees).astype(jnp.int32), axis=2)
    chosen = jnp.sum((same & (branch_ids[:, None, :] == 1)).astype(jnp.int32), axis=2)
    own_start = jnp.sum(jnp.where(same, starts[:, :, None], 0), axis=1)
    own_chosen = jnp.sum(jnp.where(same, chosen[:, :, None], 0), axis=1)
    skipped = jnp.where(branch_ids == 2, own_chosen, 0)
    return positions - own_start - skipped


def by_span(values, span_order):
    micro_count, seq_len = values.shape
    spans = seq_len // SPAN
    blocks = values.reshape(micro_count, 1, spans, SPAN)
    picks = span_order[:, :, None] == jnp.arange(spans, dtype=jnp.int32)[None, None, :]
    chosen = jnp.where(picks[..., None], blocks, 0)
    return jnp.sum(chosen, axis=2).reshape(micro_count, seq_len)


def ring_gather(value, shift):
    ahead = shift(value, 1)
    behind = shift(value, -1)
    width = value.shape[1] // 2
    far = jnp.concatenate(
        [shift(ahead[:, :width], 1), shift(behind[:, width:], -1)], axis=1
    )
    return [value, ahead, behind, far]


RING_OFFSETS = (0, -1, 1, 2)


def torus_gather(value, side):
    def shifter(along_z):
        def shift(piece, by):
            pairs = []
            for z in range(side):
                for x in range(side):
                    if along_z:
                        pairs.append((z * side + x, ((z + by) % side) * side + x))
                    else:
                        pairs.append((z * side + x, z * side + (x + by) % side))
            return lax.ppermute(piece, "seq", pairs)

        return shift

    shift_z = shifter(True)
    shift_x = shifter(False)
    rows = value.shape[0]
    width = value.shape[1] // 2
    row_a = jnp.concatenate(ring_gather(value[:, :width], shift_x), axis=0)
    full_a = jnp.concatenate(ring_gather(row_a, shift_z), axis=0)
    col_b = jnp.concatenate(ring_gather(value[:, width:], shift_z), axis=0)
    pieces_b = ring_gather(col_b, shift_x)
    full_b = jnp.stack(pieces_b, axis=0).reshape(side, side, rows, width)
    full_b = full_b.transpose(1, 0, 2, 3).reshape(side * side * rows, width)
    return jnp.concatenate([full_a, full_b], axis=1)


def torus_order(values, shard_id, side, rows):
    micro_count = values.shape[0]
    z = shard_id // side
    x = shard_id % side
    blocks = values.reshape(micro_count, side, side, rows)
    blocks = jnp.roll(blocks, -z, axis=1)
    blocks = jnp.roll(blocks, -x, axis=2)
    picks = [o % side for o in RING_OFFSETS]
    blocks = jnp.stack([blocks[:, p] for p in picks], axis=1)
    blocks = jnp.stack([blocks[:, :, q] for q in picks], axis=2)
    return blocks.reshape(micro_count, side * side * rows)


CHUNK = 128


def attention_kernel(need_ref, q_ref, k_ref, v_ref, bias_ref, res_ref, o_ref, s_scr, m_scr, l_scr, acc_scr):
    ratio = HQ // HK
    scale = 1.0 / math.sqrt(HD)
    chunks = k_ref.shape[0] // CHUNK
    m_scr[...] = jnp.full(m_scr.shape, -jnp.inf, jnp.float32)
    l_scr[...] = jnp.zeros(l_scr.shape, jnp.float32)
    acc_scr[...] = jnp.zeros(acc_scr.shape, jnp.float32)

    def score_pass(c, carry):
        @pl.when(need_ref[c] > 0)
        def _():
            keys = k_ref[pl.ds(c * CHUNK, CHUNK), :]
            bias = bias_ref[:, pl.ds(c * CHUNK, CHUNK)]
            for g in range(ratio):
                scores = lax.dot_general(
                    q_ref[:, g * HD : (g + 1) * HD],
                    keys,
                    (((1,), (1,)), ((), ())),
                    preferred_element_type=jnp.float32,
                )
                masked = scores * scale + bias
                s_scr[g, :, pl.ds(c * CHUNK, CHUNK)] = masked
                m_scr[g] = jnp.maximum(m_scr[g], jnp.max(masked, axis=-1, keepdims=True))

        return carry

    lax.fori_loop(0, chunks, score_pass, 0)

    def weight_pass(c, carry):
        @pl.when(need_ref[c] > 0)
        def _():
            values = v_ref[pl.ds(c * CHUNK, CHUNK), :]
            for g in range(ratio):
                weights = jnp.exp(s_scr[g, :, pl.ds(c * CHUNK, CHUNK)] - m_scr[g])
                l_scr[g] = l_scr[g] + jnp.sum(weights, axis=-1, keepdims=True)
                acc_scr[g] = acc_scr[g] + jnp.dot(
                    weights.astype(jnp.bfloat16), values, preferred_element_type=jnp.float32
                )

        return carry

    lax.fori_loop(0, chunks, weight_pass, 0)
    for g in range(ratio):
        cols = slice(g * HD, (g + 1) * HD)
        attended = (acc_scr[g] / l_scr[g]).astype(jnp.bfloat16)
        o_ref[:, cols] = (
            res_ref[:, cols].astype(jnp.float32) + attended.astype(jnp.float32)
        ).astype(o_ref.dtype)


def attention(need, turned, kv_all, bias, residual):
    rows, width = turned.shape
    keys_len = kv_all.shape[0]
    group = width // HK
    ratio = HQ // HK
    grid_spec = pltpu.PrefetchScalarGridSpec(
        num_scalar_prefetch=1,
        grid=(HK,),
        in_specs=[
            pl.BlockSpec((rows, group), lambda k, n: (0, k)),
            pl.BlockSpec((keys_len, HD), lambda k, n: (0, k)),
            pl.BlockSpec((keys_len, HD), lambda k, n: (0, HK + k)),
            pl.BlockSpec((rows, keys_len), lambda k, n: (0, 0)),
            pl.BlockSpec((rows, group), lambda k, n: (0, k)),
        ],
        out_specs=pl.BlockSpec((rows, group), lambda k, n: (0, k)),
        scratch_shapes=[
            pltpu.VMEM((ratio, rows, keys_len), jnp.float32),
            pltpu.VMEM((ratio, rows, 1), jnp.float32),
            pltpu.VMEM((ratio, rows, 1), jnp.float32),
            pltpu.VMEM((ratio, rows, HD), jnp.float32),
        ],
    )
    return pl.pallas_call(
        attention_kernel,
        grid_spec=grid_spec,
        out_shape=jax.ShapeDtypeStruct((rows, width), jnp.bfloat16),
    )(need, turned, kv_all, kv_all, bias, residual)


def local(hidden, queries, gain, key_weight, value_weight, tree_ids, branch_ids, span_order):
    section_id = lax.axis_index("section")
    shard_id = lax.axis_index("seq")
    section_count = lax.axis_size("section")
    micro_count, row_count, model_width = hidden.shape
    seq_len = tree_ids.shape[1]
    rotary_all = tree_positions(tree_ids, branch_ids)
    stored_ids = jnp.arange(seq_len, dtype=jnp.int32)
    packed_all = jnp.repeat(span_order, SPAN, axis=1) * SPAN + stored_ids % SPAN
    key_tree = by_span(tree_ids, span_order)
    key_branch = by_span(branch_ids, span_order)
    key_rotary = by_span(rotary_all, span_order)
    first_row = shard_id * row_count
    own_packed = lax.dynamic_slice_in_dim(packed_all, first_row, row_count, 1)
    own_tree = lax.dynamic_slice_in_dim(key_tree, first_row, row_count, 1)
    own_branch = lax.dynamic_slice_in_dim(key_branch, first_row, row_count, 1)
    own_rotary = lax.dynamic_slice_in_dim(key_rotary, first_row, row_count, 1)
    seq_count = lax.axis_size("seq")
    side = math.isqrt(seq_count)
    order_tree = torus_order(key_tree, shard_id, side, row_count)
    order_branch = torus_order(key_branch, shard_id, side, row_count)
    order_packed = torus_order(packed_all, shard_id, side, row_count)
    allowed = (
        (own_tree[:, :, None] == order_tree[:, None, :])
        & (order_packed[:, None, :] <= own_packed[:, :, None])
        & ((order_branch[:, None, :] == 0) | (order_branch[:, None, :] == own_branch[:, :, None]))
    )
    bias_all = jnp.where(allowed, 0.0, -jnp.inf).astype(jnp.float32)
    need_all = jnp.any(
        allowed.reshape(micro_count, row_count, seq_len // CHUNK, CHUNK), axis=(1, 3)
    ).astype(jnp.int32)
    angles = own_rotary.astype(jnp.float32)[..., None] * frequencies()
    cos_all = jnp.cos(angles)
    sin_all = jnp.sin(angles)
    gain_row = gain[0]
    key_mat = key_weight[0]
    value_mat = value_weight[0]
    kv_mat = jnp.concatenate([key_mat, value_mat], axis=1)

    def run_layer(current, mb):
        cosine = lax.dynamic_index_in_dim(cos_all, mb, 0, keepdims=False)
        sine_part = lax.dynamic_index_in_dim(sin_all, mb, 0, keepdims=False)
        bias = lax.dynamic_index_in_dim(bias_all, mb, 0, keepdims=False)
        need = lax.dynamic_index_in_dim(need_all, mb, 0, keepdims=False)
        widened = current.astype(jnp.float32)
        norm_scale = lax.rsqrt(jnp.mean(widened * widened, axis=-1, keepdims=True) + 1e-05)
        normed = (widened * norm_scale * gain_row).astype(jnp.bfloat16)
        kv_proj = jnp.dot(normed, kv_mat, preferred_element_type=jnp.float32)
        key_proj = kv_proj[:, : HK * HD].reshape(row_count, HK, HD)
        key_rows = (
            rotate(key_proj, cosine[:, None, :], sine_part[:, None, :])
            .astype(jnp.bfloat16)
            .reshape(row_count, HK * HD)
        )
        value_rows = kv_proj[:, HK * HD :].astype(jnp.bfloat16)
        kv_rows = jnp.concatenate([key_rows, value_rows], axis=1)
        kv_all = torus_gather(kv_rows, side)
        query_local = lax.dynamic_index_in_dim(queries[0], mb, 0, keepdims=False)
        turned = (
            rotate(
                query_local.astype(jnp.float32).reshape(row_count, HQ, HD),
                cosine[:, None, :],
                sine_part[:, None, :],
            )
            .astype(jnp.bfloat16)
            .reshape(row_count, HQ * HD)
        )
        return attention(need, turned, kv_all, bias, current)

    tick_count = section_count + micro_count - 1

    def advance(step_id, state_pair):
        previous, outputs = state_pair
        incoming = from_behind(previous, "section", 1)
        first_mb = step_id - section_id
        active = (first_mb >= 0) & (first_mb < micro_count)
        start_at = jnp.clip(first_mb, 0, micro_count - 1)
        entering = lax.dynamic_index_in_dim(hidden, start_at, 0, keepdims=False)
        current = jnp.where(section_id == 0, entering, incoming)
        computed = run_layer(current, start_at)
        result = jnp.where(active, computed, jnp.zeros_like(computed))
        stored = lax.dynamic_update_index_in_dim(outputs, result, start_at, 0)
        outputs = jnp.where(active, stored, outputs)
        return (result, outputs)

    empty_pass = jnp.zeros((row_count, model_width), jnp.bfloat16)
    empty_out = jnp.zeros((micro_count, row_count, model_width), jnp.bfloat16)
    final_pass, outputs = lax.fori_loop(0, tick_count, advance, (empty_pass, empty_out))
    return outputs[None]


def solution(mesh):
    placed = (
        P(None, "seq", None),
        P("section", None, "seq", None),
        P("section", None),
        P("section", None, None),
        P("section", None, None),
        P(),
        P(),
        P(),
    )
    return jax.shard_map(
        local,
        mesh=mesh,
        in_specs=placed,
        out_specs=P("section", None, "seq", None),
        check_vma=False,
    )
```

```python
import math

import jax
import jax.numpy as jnp
from jax import lax
from jax.experimental import pallas as pl
from jax.experimental.pallas import tpu as pltpu
from jax.sharding import PartitionSpec as P

HQ = 32
HK = 4
HD = 128
SPAN = 64


rope_base = 500000.0


def from_behind(value, axis, by):
    size = lax.axis_size(axis)
    pairs = [(i, i + by) for i in range(size) if 0 <= i + by < size]
    return lax.ppermute(value, axis, pairs)


def frequencies():
    exponent = jnp.arange(HD // 2, dtype=jnp.float32) * (2.0 / HD)
    return jnp.power(jnp.float32(rope_base), -exponent)


def rotate(vectors, cosine, sine_part):
    half_dim = vectors.shape[-1] // 2
    lower_half = vectors[..., :half_dim]
    upper_half = vectors[..., half_dim:]
    return jnp.concatenate(
        [
            lower_half * cosine - upper_half * sine_part,
            upper_half * cosine + lower_half * sine_part,
        ],
        axis=-1,
    )


def tree_positions(tree_ids, branch_ids):
    trees = jnp.arange(8, dtype=jnp.int32)[None, :, None]
    positions = jnp.arange(tree_ids.shape[1], dtype=jnp.int32)[None, :]
    same = tree_ids[:, None, :] == trees
    starts = jnp.sum((tree_ids[:, None, :] < trees).astype(jnp.int32), axis=2)
    chosen = jnp.sum((same & (branch_ids[:, None, :] == 1)).astype(jnp.int32), axis=2)
    own_start = jnp.sum(jnp.where(same, starts[:, :, None], 0), axis=1)
    own_chosen = jnp.sum(jnp.where(same, chosen[:, :, None], 0), axis=1)
    skipped = jnp.where(branch_ids == 2, own_chosen, 0)
    return positions - own_start - skipped


def by_span(values, span_order):
    micro_count, seq_len = values.shape
    spans = seq_len // SPAN
    blocks = values.reshape(micro_count, 1, spans, SPAN)
    picks = span_order[:, :, None] == jnp.arange(spans, dtype=jnp.int32)[None, None, :]
    chosen = jnp.where(picks[..., None], blocks, 0)
    return jnp.sum(chosen, axis=2).reshape(micro_count, seq_len)


def ring_gather(value, shift):
    ahead = shift(value, 1)
    behind = shift(value, -1)
    far = shift(ahead, 1)
    return [value, ahead, behind, far]


RING_OFFSETS = (0, -1, 1, 2)


def torus_gather(value, side):
    def shifter(along_z):
        def shift(piece, by):
            pairs = []
            for z in range(side):
                for x in range(side):
                    if along_z:
                        pairs.append((z * side + x, ((z + by) % side) * side + x))
                    else:
                        pairs.append((z * side + x, z * side + (x + by) % side))
            return lax.ppermute(piece, "seq", pairs)

        return shift

    shift_z = shifter(True)
    shift_x = shifter(False)
    rows = value.shape[0]
    width = value.shape[1] // 2
    row_a = jnp.concatenate(ring_gather(value[:, :width], shift_x), axis=0)
    full_a = jnp.concatenate(ring_gather(row_a, shift_z), axis=0)
    col_b = jnp.concatenate(ring_gather(value[:, width:], shift_z), axis=0)
    pieces_b = ring_gather(col_b, shift_x)
    full_b = jnp.stack(pieces_b, axis=0).reshape(side, side, rows, width)
    full_b = full_b.transpose(1, 0, 2, 3).reshape(side * side * rows, width)
    return jnp.concatenate([full_a, full_b], axis=1)


def torus_order(values, shard_id, side, rows):
    micro_count = values.shape[0]
    z = shard_id // side
    x = shard_id % side
    blocks = values.reshape(micro_count, side, side, rows)
    blocks = jnp.roll(blocks, -z, axis=1)
    blocks = jnp.roll(blocks, -x, axis=2)
    picks = [o % side for o in RING_OFFSETS]
    blocks = jnp.stack([blocks[:, p] for p in picks], axis=1)
    blocks = jnp.stack([blocks[:, :, q] for q in picks], axis=2)
    return blocks.reshape(micro_count, side * side * rows)


def attention_kernel(q_ref, k_ref, v_ref, bias_ref, res_ref, o_ref):
    ratio = HQ // HK
    scale = 1.0 / math.sqrt(HD)
    keys = k_ref[...]
    values = v_ref[...]
    bias = bias_ref[...]
    for g in range(ratio):
        cols = slice(g * HD, (g + 1) * HD)
        scores = lax.dot_general(
            q_ref[:, cols],
            keys,
            (((1,), (1,)), ((), ())),
            preferred_element_type=jnp.float32,
        )
        masked = scores * scale + bias
        row_top = jnp.max(masked, axis=-1, keepdims=True)
        weights = jnp.exp(masked - row_top)
        denominator = jnp.sum(weights, axis=-1, keepdims=True)
        summed = jnp.dot(
            weights.astype(jnp.bfloat16), values, preferred_element_type=jnp.float32
        )
        attended = (summed / denominator).astype(jnp.bfloat16)
        o_ref[:, cols] = (
            res_ref[:, cols].astype(jnp.float32) + attended.astype(jnp.float32)
        ).astype(o_ref.dtype)


def attention(turned, kv_all, bias, residual):
    rows, width = turned.shape
    keys_len = kv_all.shape[0]
    group = width // HK
    return pl.pallas_call(
        attention_kernel,
        grid=(HK,),
        in_specs=[
            pl.BlockSpec((rows, group), lambda k: (0, k)),
            pl.BlockSpec((keys_len, HD), lambda k: (0, k)),
            pl.BlockSpec((keys_len, HD), lambda k: (0, HK + k)),
            pl.BlockSpec((rows, keys_len), lambda k: (0, 0)),
            pl.BlockSpec((rows, group), lambda k: (0, k)),
        ],
        out_specs=pl.BlockSpec((rows, group), lambda k: (0, k)),
        out_shape=jax.ShapeDtypeStruct((rows, width), jnp.bfloat16),
    )(turned, kv_all, kv_all, bias, residual)


def local(hidden, queries, gain, key_weight, value_weight, tree_ids, branch_ids, span_order):
    section_id = lax.axis_index("section")
    shard_id = lax.axis_index("seq")
    section_count = lax.axis_size("section")
    micro_count, row_count, model_width = hidden.shape
    seq_len = tree_ids.shape[1]
    rotary_all = tree_positions(tree_ids, branch_ids)
    stored_ids = jnp.arange(seq_len, dtype=jnp.int32)
    packed_all = jnp.repeat(span_order, SPAN, axis=1) * SPAN + stored_ids % SPAN
    key_tree = by_span(tree_ids, span_order)
    key_branch = by_span(branch_ids, span_order)
    key_rotary = by_span(rotary_all, span_order)
    first_row = shard_id * row_count
    own_packed = lax.dynamic_slice_in_dim(packed_all, first_row, row_count, 1)
    own_tree = lax.dynamic_slice_in_dim(key_tree, first_row, row_count, 1)
    own_branch = lax.dynamic_slice_in_dim(key_branch, first_row, row_count, 1)
    own_rotary = lax.dynamic_slice_in_dim(key_rotary, first_row, row_count, 1)
    seq_count = lax.axis_size("seq")
    side = math.isqrt(seq_count)
    order_tree = torus_order(key_tree, shard_id, side, row_count)
    order_branch = torus_order(key_branch, shard_id, side, row_count)
    order_packed = torus_order(packed_all, shard_id, side, row_count)
    allowed = (
        (own_tree[:, :, None] == order_tree[:, None, :])
        & (order_packed[:, None, :] <= own_packed[:, :, None])
        & ((order_branch[:, None, :] == 0) | (order_branch[:, None, :] == own_branch[:, :, None]))
    )
    bias_all = jnp.where(allowed, 0.0, -jnp.inf).astype(jnp.float32)
    angles = own_rotary.astype(jnp.float32)[..., None] * frequencies()
    cos_all = jnp.cos(angles)
    sin_all = jnp.sin(angles)
    gain_row = gain[0]
    key_mat = key_weight[0]
    value_mat = value_weight[0]
    kv_mat = jnp.concatenate([key_mat, value_mat], axis=1)

    def run_layer(current, mb):
        cosine = lax.dynamic_index_in_dim(cos_all, mb, 0, keepdims=False)
        sine_part = lax.dynamic_index_in_dim(sin_all, mb, 0, keepdims=False)
        bias = lax.dynamic_index_in_dim(bias_all, mb, 0, keepdims=False)
        widened = current.astype(jnp.float32)
        norm_scale = lax.rsqrt(jnp.mean(widened * widened, axis=-1, keepdims=True) + 1e-05)
        normed = (widened * norm_scale * gain_row).astype(jnp.bfloat16)
        kv_proj = jnp.dot(normed, kv_mat, preferred_element_type=jnp.float32)
        key_proj = kv_proj[:, : HK * HD].reshape(row_count, HK, HD)
        key_rows = (
            rotate(key_proj, cosine[:, None, :], sine_part[:, None, :])
            .astype(jnp.bfloat16)
            .reshape(row_count, HK * HD)
        )
        value_rows = kv_proj[:, HK * HD :].astype(jnp.bfloat16)
        kv_rows = jnp.concatenate([key_rows, value_rows], axis=1)
        kv_all = torus_gather(kv_rows, side)
        query_local = lax.dynamic_index_in_dim(queries[0], mb, 0, keepdims=False)
        turned = (
            rotate(
                query_local.astype(jnp.float32).reshape(row_count, HQ, HD),
                cosine[:, None, :],
                sine_part[:, None, :],
            )
            .astype(jnp.bfloat16)
            .reshape(row_count, HQ * HD)
        )
        return attention(turned, kv_all, bias, current)

    tick_count = section_count + micro_count - 1

    def advance(step_id, state_pair):
        previous, outputs = state_pair
        incoming = from_behind(previous, "section", 1)
        first_mb = step_id - section_id
        active = (first_mb >= 0) & (first_mb < micro_count)
        start_at = jnp.clip(first_mb, 0, micro_count - 1)
        entering = lax.dynamic_index_in_dim(hidden, start_at, 0, keepdims=False)
        current = jnp.where(section_id == 0, entering, incoming)
        computed = run_layer(current, start_at)
        result = jnp.where(active, computed, jnp.zeros_like(computed))
        stored = lax.dynamic_update_index_in_dim(outputs, result, start_at, 0)
        outputs = jnp.where(active, stored, outputs)
        return (result, outputs)

    empty_pass = jnp.zeros((row_count, model_width), jnp.bfloat16)
    empty_out = jnp.zeros((micro_count, row_count, model_width), jnp.bfloat16)
    final_pass, outputs = lax.fori_loop(0, tick_count, advance, (empty_pass, empty_out))
    return outputs[None]


def solution(mesh):
    placed = (
        P(None, "seq", None),
        P("section", None, "seq", None),
        P("section", None),
        P("section", None, None),
        P("section", None, None),
        P(),
        P(),
        P(),
    )
    return jax.shard_map(
        local,
        mesh=mesh,
        in_specs=placed,
        out_specs=P("section", None, "seq", None),
        check_vma=False,
    )
```

```python
import math

import jax
import jax.numpy as jnp
from jax import lax
from jax.experimental import pallas as pl
from jax.experimental.pallas import tpu as pltpu
from jax.sharding import PartitionSpec as P

HQ = 32
HK = 4
HD = 128
SPAN = 64


rope_base = 500000.0


def from_behind(value, axis, by):
    size = lax.axis_size(axis)
    pairs = [(i, i + by) for i in range(size) if 0 <= i + by < size]
    return lax.ppermute(value, axis, pairs)


def frequencies():
    exponent = jnp.arange(HD // 2, dtype=jnp.float32) * (2.0 / HD)
    return jnp.power(jnp.float32(rope_base), -exponent)


def rotate(vectors, cosine, sine_part):
    half_dim = vectors.shape[-1] // 2
    lower_half = vectors[..., :half_dim]
    upper_half = vectors[..., half_dim:]
    return jnp.concatenate(
        [
            lower_half * cosine - upper_half * sine_part,
            upper_half * cosine + lower_half * sine_part,
        ],
        axis=-1,
    )


def tree_positions(tree_ids, branch_ids):
    trees = jnp.arange(8, dtype=jnp.int32)[None, :, None]
    positions = jnp.arange(tree_ids.shape[1], dtype=jnp.int32)[None, :]
    same = tree_ids[:, None, :] == trees
    starts = jnp.sum((tree_ids[:, None, :] < trees).astype(jnp.int32), axis=2)
    chosen = jnp.sum((same & (branch_ids[:, None, :] == 1)).astype(jnp.int32), axis=2)
    own_start = jnp.sum(jnp.where(same, starts[:, :, None], 0), axis=1)
    own_chosen = jnp.sum(jnp.where(same, chosen[:, :, None], 0), axis=1)
    skipped = jnp.where(branch_ids == 2, own_chosen, 0)
    return positions - own_start - skipped


def by_span(values, span_order):
    micro_count, seq_len = values.shape
    spans = seq_len // SPAN
    blocks = values.reshape(micro_count, 1, spans, SPAN)
    picks = span_order[:, :, None] == jnp.arange(spans, dtype=jnp.int32)[None, None, :]
    chosen = jnp.where(picks[..., None], blocks, 0)
    return jnp.sum(chosen, axis=2).reshape(micro_count, seq_len)


def ring_gather(value, shift):
    ahead = shift(value, 1)
    behind = shift(value, -1)
    far = shift(ahead, 1)
    return [value, ahead, behind, far]


RING_OFFSETS = (0, -1, 1, 2)


def torus_gather(value, side):
    def shifter(along_z):
        def shift(piece, by):
            pairs = []
            for z in range(side):
                for x in range(side):
                    if along_z:
                        pairs.append((z * side + x, ((z + by) % side) * side + x))
                    else:
                        pairs.append((z * side + x, z * side + (x + by) % side))
            return lax.ppermute(piece, "seq", pairs)

        return shift

    shift_z = shifter(True)
    shift_x = shifter(False)
    rows = value.shape[0]
    width = value.shape[1] // 2
    row_a = jnp.concatenate(ring_gather(value[:, :width], shift_x), axis=0)
    full_a = jnp.concatenate(ring_gather(row_a, shift_z), axis=0)
    col_b = jnp.concatenate(ring_gather(value[:, width:], shift_z), axis=0)
    pieces_b = ring_gather(col_b, shift_x)
    full_b = jnp.stack(pieces_b, axis=0).reshape(side, side, rows, width)
    full_b = full_b.transpose(1, 0, 2, 3).reshape(side * side * rows, width)
    return jnp.concatenate([full_a, full_b], axis=1)


def torus_order(values, shard_id, side, rows):
    micro_count = values.shape[0]
    z = shard_id // side
    x = shard_id % side
    blocks = values.reshape(micro_count, side, side, rows)
    blocks = jnp.roll(blocks, -z, axis=1)
    blocks = jnp.roll(blocks, -x, axis=2)
    picks = [o % side for o in RING_OFFSETS]
    blocks = jnp.stack([blocks[:, p] for p in picks], axis=1)
    blocks = jnp.stack([blocks[:, :, q] for q in picks], axis=2)
    return blocks.reshape(micro_count, side * side * rows)


def attention_kernel(q_ref, k_ref, v_ref, bias_ref, res_ref, o_ref):
    ratio = HQ // HK
    scale = 1.0 / math.sqrt(HD)
    keys = k_ref[...]
    values = v_ref[...]
    bias = bias_ref[...]
    for g in range(ratio):
        cols = slice(g * HD, (g + 1) * HD)
        scores = lax.dot_general(
            q_ref[:, cols],
            keys,
            (((1,), (1,)), ((), ())),
            preferred_element_type=jnp.float32,
        )
        masked = scores * scale + bias
        row_top = jnp.max(masked, axis=-1, keepdims=True)
        weights = jnp.exp(masked - row_top)
        denominator = jnp.sum(weights, axis=-1, keepdims=True)
        summed = jnp.dot(
            weights.astype(jnp.bfloat16), values, preferred_element_type=jnp.float32
        )
        attended = (summed / denominator).astype(jnp.bfloat16)
        o_ref[:, cols] = (
            res_ref[:, cols].astype(jnp.float32) + attended.astype(jnp.float32)
        ).astype(o_ref.dtype)


def attention(turned, kv_all, bias, residual):
    rows, width = turned.shape
    keys_len = kv_all.shape[0]
    group = width // HK
    return pl.pallas_call(
        attention_kernel,
        grid=(HK,),
        in_specs=[
            pl.BlockSpec((rows, group), lambda k: (0, k)),
            pl.BlockSpec((keys_len, HD), lambda k: (0, k)),
            pl.BlockSpec((keys_len, HD), lambda k: (0, HK + k)),
            pl.BlockSpec((rows, keys_len), lambda k: (0, 0)),
            pl.BlockSpec((rows, group), lambda k: (0, k)),
        ],
        out_specs=pl.BlockSpec((rows, group), lambda k: (0, k)),
        out_shape=jax.ShapeDtypeStruct((rows, width), jnp.bfloat16),
    )(turned, kv_all, kv_all, bias, residual)


def local(hidden, queries, gain, key_weight, value_weight, tree_ids, branch_ids, span_order):
    section_id = lax.axis_index("section")
    shard_id = lax.axis_index("seq")
    section_count = lax.axis_size("section")
    micro_count, row_count, model_width = hidden.shape
    seq_len = tree_ids.shape[1]
    rotary_all = tree_positions(tree_ids, branch_ids)
    stored_ids = jnp.arange(seq_len, dtype=jnp.int32)
    packed_all = jnp.repeat(span_order, SPAN, axis=1) * SPAN + stored_ids % SPAN
    key_tree = by_span(tree_ids, span_order)
    key_branch = by_span(branch_ids, span_order)
    key_rotary = by_span(rotary_all, span_order)
    first_row = shard_id * row_count
    own_packed = lax.dynamic_slice_in_dim(packed_all, first_row, row_count, 1)
    own_tree = lax.dynamic_slice_in_dim(key_tree, first_row, row_count, 1)
    own_branch = lax.dynamic_slice_in_dim(key_branch, first_row, row_count, 1)
    own_rotary = lax.dynamic_slice_in_dim(key_rotary, first_row, row_count, 1)
    seq_count = lax.axis_size("seq")
    side = math.isqrt(seq_count)
    order_tree = torus_order(key_tree, shard_id, side, row_count)
    order_branch = torus_order(key_branch, shard_id, side, row_count)
    order_packed = torus_order(packed_all, shard_id, side, row_count)
    allowed = (
        (own_tree[:, :, None] == order_tree[:, None, :])
        & (order_packed[:, None, :] <= own_packed[:, :, None])
        & ((order_branch[:, None, :] == 0) | (order_branch[:, None, :] == own_branch[:, :, None]))
    )
    bias_all = jnp.where(allowed, 0.0, -jnp.inf).astype(jnp.float32)
    angles = own_rotary.astype(jnp.float32)[..., None] * frequencies()
    cos_all = jnp.cos(angles)
    sin_all = jnp.sin(angles)
    gain_row = gain[0]
    key_mat = key_weight[0]
    value_mat = value_weight[0]
    kv_mat = jnp.concatenate([key_mat, value_mat], axis=1)

    def run_layer(current, mb):
        cosine = lax.dynamic_index_in_dim(cos_all, mb, 0, keepdims=False)
        sine_part = lax.dynamic_index_in_dim(sin_all, mb, 0, keepdims=False)
        bias = lax.dynamic_index_in_dim(bias_all, mb, 0, keepdims=False)
        widened = current.astype(jnp.float32)
        norm_scale = lax.rsqrt(jnp.mean(widened * widened, axis=-1, keepdims=True) + 1e-05)
        normed = (widened * norm_scale * gain_row).astype(jnp.bfloat16)
        kv_proj = jnp.dot(normed, kv_mat, preferred_element_type=jnp.float32)
        key_proj = kv_proj[:, : HK * HD].reshape(row_count, HK, HD)
        key_rows = (
            rotate(key_proj, cosine[:, None, :], sine_part[:, None, :])
            .astype(jnp.bfloat16)
            .reshape(row_count, HK * HD)
        )
        value_rows = kv_proj[:, HK * HD :].astype(jnp.bfloat16)
        kv_rows = jnp.concatenate([key_rows, value_rows], axis=1)
        kv_all = torus_gather(kv_rows, side)
        query_local = lax.dynamic_index_in_dim(queries[0], mb, 0, keepdims=False)
        turned = (
            rotate(
                query_local.astype(jnp.float32).reshape(row_count, HQ, HD),
                cosine[:, None, :],
                sine_part[:, None, :],
            )
            .astype(jnp.bfloat16)
            .reshape(row_count, HQ * HD)
        )
        return attention(turned, kv_all, bias, current)

    tick_count = section_count + micro_count - 1

    def advance(step_id, state_pair):
        previous, outputs = state_pair
        incoming = from_behind(previous, "section", 1)
        first_mb = step_id - section_id
        active = (first_mb >= 0) & (first_mb < micro_count)
        start_at = jnp.clip(first_mb, 0, micro_count - 1)
        entering = lax.dynamic_index_in_dim(hidden, start_at, 0, keepdims=False)
        current = jnp.where(section_id == 0, entering, incoming)
        result = lax.cond(
            active,
            lambda rows: run_layer(rows, start_at),
            jnp.zeros_like,
            current,
        )
        stored = lax.dynamic_update_index_in_dim(outputs, result, start_at, 0)
        outputs = jnp.where(active, stored, outputs)
        return (result, outputs)

    empty_pass = jnp.zeros((row_count, model_width), jnp.bfloat16)
    empty_out = jnp.zeros((micro_count, row_count, model_width), jnp.bfloat16)
    final_pass, outputs = lax.fori_loop(0, tick_count, advance, (empty_pass, empty_out))
    return outputs[None]


def solution(mesh):
    placed = (
        P(None, "seq", None),
        P("section", None, "seq", None),
        P("section", None),
        P("section", None, None),
        P("section", None, None),
        P(),
        P(),
        P(),
    )
    return jax.shard_map(
        local,
        mesh=mesh,
        in_specs=placed,
        out_specs=P("section", None, "seq", None),
        check_vma=False,
    )
```

```python
import math

import jax
import jax.numpy as jnp
from jax import lax
from jax.experimental import pallas as pl
from jax.experimental.pallas import tpu as pltpu
from jax.sharding import PartitionSpec as P

HQ = 32
HK = 4
HD = 128
SPAN = 64


rope_base = 500000.0


def from_behind(value, axis, by):
    size = lax.axis_size(axis)
    pairs = [(i, i + by) for i in range(size) if 0 <= i + by < size]
    return lax.ppermute(value, axis, pairs)


def frequencies():
    exponent = jnp.arange(HD // 2, dtype=jnp.float32) * (2.0 / HD)
    return jnp.power(jnp.float32(rope_base), -exponent)


def rotate(vectors, cosine, sine_part):
    half_dim = vectors.shape[-1] // 2
    lower_half = vectors[..., :half_dim]
    upper_half = vectors[..., half_dim:]
    return jnp.concatenate(
        [
            lower_half * cosine - upper_half * sine_part,
            upper_half * cosine + lower_half * sine_part,
        ],
        axis=-1,
    )


def tree_positions(tree_ids, branch_ids):
    trees = jnp.arange(8, dtype=jnp.int32)[None, :, None]
    positions = jnp.arange(tree_ids.shape[1], dtype=jnp.int32)[None, :]
    same = tree_ids[:, None, :] == trees
    starts = jnp.sum((tree_ids[:, None, :] < trees).astype(jnp.int32), axis=2)
    chosen = jnp.sum((same & (branch_ids[:, None, :] == 1)).astype(jnp.int32), axis=2)
    own_start = jnp.sum(jnp.where(same, starts[:, :, None], 0), axis=1)
    own_chosen = jnp.sum(jnp.where(same, chosen[:, :, None], 0), axis=1)
    skipped = jnp.where(branch_ids == 2, own_chosen, 0)
    return positions - own_start - skipped


def by_span(values, span_order):
    micro_count, seq_len = values.shape
    spans = seq_len // SPAN
    blocks = values.reshape(micro_count, 1, spans, SPAN)
    picks = span_order[:, :, None] == jnp.arange(spans, dtype=jnp.int32)[None, None, :]
    chosen = jnp.where(picks[..., None], blocks, 0)
    return jnp.sum(chosen, axis=2).reshape(micro_count, seq_len)


def ring_gather(value, shift):
    ahead = shift(value, 1)
    behind = shift(value, -1)
    far = shift(value, 2)
    return [value, ahead, behind, far]


RING_OFFSETS = (0, -1, 1, 2)


def torus_gather(value, side):
    def shifter(along_z):
        def shift(piece, by):
            pairs = []
            for z in range(side):
                for x in range(side):
                    if along_z:
                        pairs.append((z * side + x, ((z + by) % side) * side + x))
                    else:
                        pairs.append((z * side + x, z * side + (x + by) % side))
            return lax.ppermute(piece, "seq", pairs)

        return shift

    shift_z = shifter(True)
    shift_x = shifter(False)
    rows = value.shape[0]
    width = value.shape[1] // 2
    row_a = jnp.concatenate(ring_gather(value[:, :width], shift_x), axis=0)
    full_a = jnp.concatenate(ring_gather(row_a, shift_z), axis=0)
    col_b = jnp.concatenate(ring_gather(value[:, width:], shift_z), axis=0)
    pieces_b = ring_gather(col_b, shift_x)
    full_b = jnp.stack(pieces_b, axis=0).reshape(side, side, rows, width)
    full_b = full_b.transpose(1, 0, 2, 3).reshape(side * side * rows, width)
    return jnp.concatenate([full_a, full_b], axis=1)


def torus_order(values, shard_id, side, rows):
    micro_count = values.shape[0]
    z = shard_id // side
    x = shard_id % side
    blocks = values.reshape(micro_count, side, side, rows)
    blocks = jnp.roll(blocks, -z, axis=1)
    blocks = jnp.roll(blocks, -x, axis=2)
    picks = [o % side for o in RING_OFFSETS]
    blocks = jnp.stack([blocks[:, p] for p in picks], axis=1)
    blocks = jnp.stack([blocks[:, :, q] for q in picks], axis=2)
    return blocks.reshape(micro_count, side * side * rows)


def attention_kernel(q_ref, k_ref, v_ref, bias_ref, res_ref, o_ref):
    ratio = HQ // HK
    scale = 1.0 / math.sqrt(HD)
    keys = k_ref[...]
    values = v_ref[...]
    bias = bias_ref[...]
    for g in range(ratio):
        cols = slice(g * HD, (g + 1) * HD)
        scores = lax.dot_general(
            q_ref[:, cols],
            keys,
            (((1,), (1,)), ((), ())),
            preferred_element_type=jnp.float32,
        )
        masked = scores * scale + bias
        row_top = jnp.max(masked, axis=-1, keepdims=True)
        weights = jnp.exp(masked - row_top)
        denominator = jnp.sum(weights, axis=-1, keepdims=True)
        summed = jnp.dot(
            weights.astype(jnp.bfloat16), values, preferred_element_type=jnp.float32
        )
        attended = (summed / denominator).astype(jnp.bfloat16)
        o_ref[:, cols] = (
            res_ref[:, cols].astype(jnp.float32) + attended.astype(jnp.float32)
        ).astype(o_ref.dtype)


def attention(turned, kv_all, bias, residual):
    rows, width = turned.shape
    keys_len = kv_all.shape[0]
    group = width // HK
    return pl.pallas_call(
        attention_kernel,
        grid=(HK,),
        in_specs=[
            pl.BlockSpec((rows, group), lambda k: (0, k)),
            pl.BlockSpec((keys_len, HD), lambda k: (0, k)),
            pl.BlockSpec((keys_len, HD), lambda k: (0, HK + k)),
            pl.BlockSpec((rows, keys_len), lambda k: (0, 0)),
            pl.BlockSpec((rows, group), lambda k: (0, k)),
        ],
        out_specs=pl.BlockSpec((rows, group), lambda k: (0, k)),
        out_shape=jax.ShapeDtypeStruct((rows, width), jnp.bfloat16),
    )(turned, kv_all, kv_all, bias, residual)


def local(hidden, queries, gain, key_weight, value_weight, tree_ids, branch_ids, span_order):
    section_id = lax.axis_index("section")
    shard_id = lax.axis_index("seq")
    section_count = lax.axis_size("section")
    micro_count, row_count, model_width = hidden.shape
    seq_len = tree_ids.shape[1]
    rotary_all = tree_positions(tree_ids, branch_ids)
    stored_ids = jnp.arange(seq_len, dtype=jnp.int32)
    packed_all = jnp.repeat(span_order, SPAN, axis=1) * SPAN + stored_ids % SPAN
    key_tree = by_span(tree_ids, span_order)
    key_branch = by_span(branch_ids, span_order)
    key_rotary = by_span(rotary_all, span_order)
    first_row = shard_id * row_count
    own_packed = lax.dynamic_slice_in_dim(packed_all, first_row, row_count, 1)
    own_tree = lax.dynamic_slice_in_dim(key_tree, first_row, row_count, 1)
    own_branch = lax.dynamic_slice_in_dim(key_branch, first_row, row_count, 1)
    own_rotary = lax.dynamic_slice_in_dim(key_rotary, first_row, row_count, 1)
    seq_count = lax.axis_size("seq")
    side = math.isqrt(seq_count)
    order_tree = torus_order(key_tree, shard_id, side, row_count)
    order_branch = torus_order(key_branch, shard_id, side, row_count)
    order_packed = torus_order(packed_all, shard_id, side, row_count)
    allowed = (
        (own_tree[:, :, None] == order_tree[:, None, :])
        & (order_packed[:, None, :] <= own_packed[:, :, None])
        & ((order_branch[:, None, :] == 0) | (order_branch[:, None, :] == own_branch[:, :, None]))
    )
    bias_all = jnp.where(allowed, 0.0, -jnp.inf).astype(jnp.float32)
    angles = own_rotary.astype(jnp.float32)[..., None] * frequencies()
    cos_all = jnp.cos(angles)
    sin_all = jnp.sin(angles)
    gain_row = gain[0]
    key_mat = key_weight[0]
    value_mat = value_weight[0]
    kv_mat = jnp.concatenate([key_mat, value_mat], axis=1)

    def run_layer(current, mb):
        cosine = lax.dynamic_index_in_dim(cos_all, mb, 0, keepdims=False)
        sine_part = lax.dynamic_index_in_dim(sin_all, mb, 0, keepdims=False)
        bias = lax.dynamic_index_in_dim(bias_all, mb, 0, keepdims=False)
        widened = current.astype(jnp.float32)
        norm_scale = lax.rsqrt(jnp.mean(widened * widened, axis=-1, keepdims=True) + 1e-05)
        normed = (widened * norm_scale * gain_row).astype(jnp.bfloat16)
        kv_proj = jnp.dot(normed, kv_mat, preferred_element_type=jnp.float32)
        key_proj = kv_proj[:, : HK * HD].reshape(row_count, HK, HD)
        key_rows = (
            rotate(key_proj, cosine[:, None, :], sine_part[:, None, :])
            .astype(jnp.bfloat16)
            .reshape(row_count, HK * HD)
        )
        value_rows = kv_proj[:, HK * HD :].astype(jnp.bfloat16)
        kv_rows = jnp.concatenate([key_rows, value_rows], axis=1)
        kv_all = torus_gather(kv_rows, side)
        query_local = lax.dynamic_index_in_dim(queries[0], mb, 0, keepdims=False)
        turned = (
            rotate(
                query_local.astype(jnp.float32).reshape(row_count, HQ, HD),
                cosine[:, None, :],
                sine_part[:, None, :],
            )
            .astype(jnp.bfloat16)
            .reshape(row_count, HQ * HD)
        )
        return attention(turned, kv_all, bias, current)

    tick_count = section_count + micro_count - 1

    def advance(step_id, state_pair):
        previous, outputs = state_pair
        incoming = from_behind(previous, "section", 1)
        first_mb = step_id - section_id
        active = (first_mb >= 0) & (first_mb < micro_count)
        start_at = jnp.clip(first_mb, 0, micro_count - 1)
        entering = lax.dynamic_index_in_dim(hidden, start_at, 0, keepdims=False)
        current = jnp.where(section_id == 0, entering, incoming)
        result = lax.cond(
            active,
            lambda rows: run_layer(rows, start_at),
            jnp.zeros_like,
            current,
        )
        stored = lax.dynamic_update_index_in_dim(outputs, result, start_at, 0)
        outputs = jnp.where(active, stored, outputs)
        return (result, outputs)

    empty_pass = jnp.zeros((row_count, model_width), jnp.bfloat16)
    empty_out = jnp.zeros((micro_count, row_count, model_width), jnp.bfloat16)
    final_pass, outputs = lax.fori_loop(0, tick_count, advance, (empty_pass, empty_out))
    return outputs[None]


def solution(mesh):
    placed = (
        P(None, "seq", None),
        P("section", None, "seq", None),
        P("section", None),
        P("section", None, None),
        P("section", None, None),
        P(),
        P(),
        P(),
    )
    return jax.shard_map(
        local,
        mesh=mesh,
        in_specs=placed,
        out_specs=P("section", None, "seq", None),
        check_vma=False,
    )
```

```python
import math

import jax
import jax.numpy as jnp
from jax import lax
from jax.experimental import pallas as pl
from jax.experimental.pallas import tpu as pltpu
from jax.sharding import PartitionSpec as P

HQ = 32
HK = 4
HD = 128
SPAN = 64


rope_base = 500000.0


def from_behind(value, axis, by):
    size = lax.axis_size(axis)
    pairs = [(i, i + by) for i in range(size) if 0 <= i + by < size]
    return lax.ppermute(value, axis, pairs)


def frequencies():
    exponent = jnp.arange(HD // 2, dtype=jnp.float32) * (2.0 / HD)
    return jnp.power(jnp.float32(rope_base), -exponent)


def rotate(vectors, cosine, sine_part):
    half_dim = vectors.shape[-1] // 2
    lower_half = vectors[..., :half_dim]
    upper_half = vectors[..., half_dim:]
    return jnp.concatenate(
        [
            lower_half * cosine - upper_half * sine_part,
            upper_half * cosine + lower_half * sine_part,
        ],
        axis=-1,
    )


def tree_positions(tree_ids, branch_ids):
    trees = jnp.arange(8, dtype=jnp.int32)[None, :, None]
    positions = jnp.arange(tree_ids.shape[1], dtype=jnp.int32)[None, :]
    same = tree_ids[:, None, :] == trees
    starts = jnp.sum((tree_ids[:, None, :] < trees).astype(jnp.int32), axis=2)
    chosen = jnp.sum((same & (branch_ids[:, None, :] == 1)).astype(jnp.int32), axis=2)
    own_start = jnp.sum(jnp.where(same, starts[:, :, None], 0), axis=1)
    own_chosen = jnp.sum(jnp.where(same, chosen[:, :, None], 0), axis=1)
    skipped = jnp.where(branch_ids == 2, own_chosen, 0)
    return positions - own_start - skipped


def by_span(values, span_order):
    micro_count, seq_len = values.shape
    spans = seq_len // SPAN
    blocks = values.reshape(micro_count, 1, spans, SPAN)
    picks = span_order[:, :, None] == jnp.arange(spans, dtype=jnp.int32)[None, None, :]
    chosen = jnp.where(picks[..., None], blocks, 0)
    return jnp.sum(chosen, axis=2).reshape(micro_count, seq_len)


def ring_gather(value, shift):
    ahead = shift(value, 1)
    behind = shift(value, -1)
    far = shift(ahead, 1)
    return [value, ahead, behind, far]


RING_OFFSETS = (0, -1, 1, 2)


def torus_gather(value, side):
    def shifter(along_z):
        def shift(piece, by):
            pairs = []
            for z in range(side):
                for x in range(side):
                    if along_z:
                        pairs.append((z * side + x, ((z + by) % side) * side + x))
                    else:
                        pairs.append((z * side + x, z * side + (x + by) % side))
            return lax.ppermute(piece, "seq", pairs)

        return shift

    shift_z = shifter(True)
    shift_x = shifter(False)
    rows = value.shape[0]
    width = value.shape[1] // 2
    row_a = jnp.concatenate(ring_gather(value[:, :width], shift_x), axis=0)
    pieces_a = ring_gather(row_a, shift_z)
    col_b = jnp.concatenate(ring_gather(value[:, width:], shift_z), axis=0)
    pieces_b = ring_gather(col_b, shift_x)
    return pieces_a, pieces_b


def torus_order(values, shard_id, side, rows):
    micro_count = values.shape[0]
    z = shard_id // side
    x = shard_id % side
    blocks = values.reshape(micro_count, side, side, rows)
    blocks = jnp.roll(blocks, -z, axis=1)
    blocks = jnp.roll(blocks, -x, axis=2)
    picks = [o % side for o in RING_OFFSETS]
    blocks = jnp.stack([blocks[:, p] for p in picks], axis=1)
    blocks = jnp.stack([blocks[:, :, q] for q in picks], axis=2)
    return blocks.reshape(micro_count, side * side * rows)


def attention_kernel(q_ref, *refs):
    side = len(RING_OFFSETS)
    key_refs = refs[:side]
    value_refs = refs[side : 2 * side]
    bias_ref, res_ref, o_ref = refs[2 * side :]
    ratio = HQ // HK
    scale = 1.0 / math.sqrt(HD)
    piece = key_refs[0].shape[0]
    rows = piece // side
    for g in range(ratio):
        cols = slice(g * HD, (g + 1) * HD)
        query = q_ref[:, cols]
        masked = []
        for p in range(side):
            scores = lax.dot_general(
                query,
                key_refs[p][...],
                (((1,), (1,)), ((), ())),
                preferred_element_type=jnp.float32,
            )
            masked.append(scores * scale + bias_ref[:, p * piece : (p + 1) * piece])
        row_top = jnp.max(masked[0], axis=-1, keepdims=True)
        for p in range(1, side):
            row_top = jnp.maximum(row_top, jnp.max(masked[p], axis=-1, keepdims=True))
        weights = [jnp.exp(m - row_top) for m in masked]
        denominator = jnp.sum(weights[0], axis=-1, keepdims=True)
        for p in range(1, side):
            denominator = denominator + jnp.sum(weights[p], axis=-1, keepdims=True)
        rounded = [w.astype(jnp.bfloat16) for w in weights]
        summed = None
        for q in range(side):
            picked = jnp.concatenate(
                [rounded[p][:, q * rows : (q + 1) * rows] for p in range(side)], axis=1
            )
            part = jnp.dot(picked, value_refs[q][...], preferred_element_type=jnp.float32)
            summed = part if summed is None else summed + part
        attended = (summed / denominator).astype(jnp.bfloat16)
        o_ref[:, cols] = (
            res_ref[:, cols].astype(jnp.float32) + attended.astype(jnp.float32)
        ).astype(o_ref.dtype)


def attention(turned, pieces_a, pieces_b, bias, residual):
    rows, width = turned.shape
    piece = pieces_a[0].shape[0]
    keys_len = bias.shape[1]
    group = width // HK
    piece_spec = pl.BlockSpec((piece, HD), lambda k: (0, k))
    return pl.pallas_call(
        attention_kernel,
        grid=(HK,),
        in_specs=[pl.BlockSpec((rows, group), lambda k: (0, k))]
        + [piece_spec] * (len(pieces_a) + len(pieces_b))
        + [
            pl.BlockSpec((rows, keys_len), lambda k: (0, 0)),
            pl.BlockSpec((rows, group), lambda k: (0, k)),
        ],
        out_specs=pl.BlockSpec((rows, group), lambda k: (0, k)),
        out_shape=jax.ShapeDtypeStruct((rows, width), jnp.bfloat16),
    )(turned, *pieces_a, *pieces_b, bias, residual)


def local(hidden, queries, gain, key_weight, value_weight, tree_ids, branch_ids, span_order):
    section_id = lax.axis_index("section")
    shard_id = lax.axis_index("seq")
    section_count = lax.axis_size("section")
    micro_count, row_count, model_width = hidden.shape
    seq_len = tree_ids.shape[1]
    rotary_all = tree_positions(tree_ids, branch_ids)
    stored_ids = jnp.arange(seq_len, dtype=jnp.int32)
    packed_all = jnp.repeat(span_order, SPAN, axis=1) * SPAN + stored_ids % SPAN
    key_tree = by_span(tree_ids, span_order)
    key_branch = by_span(branch_ids, span_order)
    key_rotary = by_span(rotary_all, span_order)
    first_row = shard_id * row_count
    own_packed = lax.dynamic_slice_in_dim(packed_all, first_row, row_count, 1)
    own_tree = lax.dynamic_slice_in_dim(key_tree, first_row, row_count, 1)
    own_branch = lax.dynamic_slice_in_dim(key_branch, first_row, row_count, 1)
    own_rotary = lax.dynamic_slice_in_dim(key_rotary, first_row, row_count, 1)
    seq_count = lax.axis_size("seq")
    side = math.isqrt(seq_count)
    order_tree = torus_order(key_tree, shard_id, side, row_count)
    order_branch = torus_order(key_branch, shard_id, side, row_count)
    order_packed = torus_order(packed_all, shard_id, side, row_count)
    allowed = (
        (own_tree[:, :, None] == order_tree[:, None, :])
        & (order_packed[:, None, :] <= own_packed[:, :, None])
        & ((order_branch[:, None, :] == 0) | (order_branch[:, None, :] == own_branch[:, :, None]))
    )
    bias_all = jnp.where(allowed, 0.0, -jnp.inf).astype(jnp.float32)
    angles = own_rotary.astype(jnp.float32)[..., None] * frequencies()
    cos_all = jnp.cos(angles)
    sin_all = jnp.sin(angles)
    gain_row = gain[0]
    key_mat = key_weight[0]
    value_mat = value_weight[0]
    kv_mat = jnp.concatenate([key_mat, value_mat], axis=1)

    def run_layer(current, mb):
        cosine = lax.dynamic_index_in_dim(cos_all, mb, 0, keepdims=False)
        sine_part = lax.dynamic_index_in_dim(sin_all, mb, 0, keepdims=False)
        bias = lax.dynamic_index_in_dim(bias_all, mb, 0, keepdims=False)
        widened = current.astype(jnp.float32)
        norm_scale = lax.rsqrt(jnp.mean(widened * widened, axis=-1, keepdims=True) + 1e-05)
        normed = (widened * norm_scale * gain_row).astype(jnp.bfloat16)
        kv_proj = jnp.dot(normed, kv_mat, preferred_element_type=jnp.float32)
        key_proj = kv_proj[:, : HK * HD].reshape(row_count, HK, HD)
        key_rows = (
            rotate(key_proj, cosine[:, None, :], sine_part[:, None, :])
            .astype(jnp.bfloat16)
            .reshape(row_count, HK * HD)
        )
        value_rows = kv_proj[:, HK * HD :].astype(jnp.bfloat16)
        kv_rows = jnp.concatenate([key_rows, value_rows], axis=1)
        pieces_a, pieces_b = torus_gather(kv_rows, side)
        query_local = lax.dynamic_index_in_dim(queries[0], mb, 0, keepdims=False)
        turned = (
            rotate(
                query_local.astype(jnp.float32).reshape(row_count, HQ, HD),
                cosine[:, None, :],
                sine_part[:, None, :],
            )
            .astype(jnp.bfloat16)
            .reshape(row_count, HQ * HD)
        )
        return attention(turned, pieces_a, pieces_b, bias, current)

    tick_count = section_count + micro_count - 1

    def advance(step_id, state_pair):
        previous, outputs = state_pair
        incoming = from_behind(previous, "section", 1)
        first_mb = step_id - section_id
        active = (first_mb >= 0) & (first_mb < micro_count)
        start_at = jnp.clip(first_mb, 0, micro_count - 1)
        entering = lax.dynamic_index_in_dim(hidden, start_at, 0, keepdims=False)
        current = jnp.where(section_id == 0, entering, incoming)
        result = lax.cond(
            active,
            lambda rows: run_layer(rows, start_at),
            jnp.zeros_like,
            current,
        )
        stored = lax.dynamic_update_index_in_dim(outputs, result, start_at, 0)
        outputs = jnp.where(active, stored, outputs)
        return (result, outputs)

    empty_pass = jnp.zeros((row_count, model_width), jnp.bfloat16)
    empty_out = jnp.zeros((micro_count, row_count, model_width), jnp.bfloat16)
    final_pass, outputs = lax.fori_loop(0, tick_count, advance, (empty_pass, empty_out))
    return outputs[None]


def solution(mesh):
    placed = (
        P(None, "seq", None),
        P("section", None, "seq", None),
        P("section", None),
        P("section", None, None),
        P("section", None, None),
        P(),
        P(),
        P(),
    )
    return jax.shard_map(
        local,
        mesh=mesh,
        in_specs=placed,
        out_specs=P("section", None, "seq", None),
        check_vma=False,
    )
```

```python
import math

import jax
import jax.numpy as jnp
from jax import lax
from jax.experimental import pallas as pl
from jax.experimental.pallas import tpu as pltpu
from jax.sharding import PartitionSpec as P

HQ = 32
HK = 4
HD = 128
SPAN = 64


rope_base = 500000.0


def from_behind(value, axis, by):
    size = lax.axis_size(axis)
    pairs = [(i, i + by) for i in range(size) if 0 <= i + by < size]
    return lax.ppermute(value, axis, pairs)


def frequencies():
    exponent = jnp.arange(HD // 2, dtype=jnp.float32) * (2.0 / HD)
    return jnp.power(jnp.float32(rope_base), -exponent)


def rotate(vectors, cosine, sine_part):
    half_dim = vectors.shape[-1] // 2
    lower_half = vectors[..., :half_dim]
    upper_half = vectors[..., half_dim:]
    return jnp.concatenate(
        [
            lower_half * cosine - upper_half * sine_part,
            upper_half * cosine + lower_half * sine_part,
        ],
        axis=-1,
    )


def tree_positions(tree_ids, branch_ids):
    trees = jnp.arange(8, dtype=jnp.int32)[None, :, None]
    positions = jnp.arange(tree_ids.shape[1], dtype=jnp.int32)[None, :]
    same = tree_ids[:, None, :] == trees
    starts = jnp.sum((tree_ids[:, None, :] < trees).astype(jnp.int32), axis=2)
    chosen = jnp.sum((same & (branch_ids[:, None, :] == 1)).astype(jnp.int32), axis=2)
    own_start = jnp.sum(jnp.where(same, starts[:, :, None], 0), axis=1)
    own_chosen = jnp.sum(jnp.where(same, chosen[:, :, None], 0), axis=1)
    skipped = jnp.where(branch_ids == 2, own_chosen, 0)
    return positions - own_start - skipped


def by_span(values, span_order):
    micro_count, seq_len = values.shape
    spans = seq_len // SPAN
    blocks = values.reshape(micro_count, 1, spans, SPAN)
    picks = span_order[:, :, None] == jnp.arange(spans, dtype=jnp.int32)[None, None, :]
    chosen = jnp.where(picks[..., None], blocks, 0)
    return jnp.sum(chosen, axis=2).reshape(micro_count, seq_len)


def ring_gather(value, shift):
    ahead = shift(value, 1)
    behind = shift(value, -1)
    far = shift(ahead, 1)
    return [value, ahead, behind, far]


RING_OFFSETS = (0, -1, 1, 2)


def torus_gather(key_rows, value_rows, side):
    def shifter(along_z):
        def shift(piece, by):
            pairs = []
            for z in range(side):
                for x in range(side):
                    if along_z:
                        pairs.append((z * side + x, ((z + by) % side) * side + x))
                    else:
                        pairs.append((z * side + x, z * side + (x + by) % side))
            return lax.ppermute(piece, "seq", pairs)

        return shift

    shift_z = shifter(True)
    shift_x = shifter(False)
    row_a = jnp.concatenate(ring_gather(key_rows, shift_x), axis=0)
    pieces_a = ring_gather(row_a, shift_z)
    col_b = jnp.concatenate(ring_gather(value_rows, shift_z), axis=0)
    pieces_b = ring_gather(col_b, shift_x)
    return pieces_a, pieces_b


def torus_order(values, shard_id, side, rows):
    micro_count = values.shape[0]
    z = shard_id // side
    x = shard_id % side
    blocks = values.reshape(micro_count, side, side, rows)
    blocks = jnp.roll(blocks, -z, axis=1)
    blocks = jnp.roll(blocks, -x, axis=2)
    picks = [o % side for o in RING_OFFSETS]
    blocks = jnp.stack([blocks[:, p] for p in picks], axis=1)
    blocks = jnp.stack([blocks[:, :, q] for q in picks], axis=2)
    return blocks.reshape(micro_count, side * side * rows)


def attention_kernel(mb_ref, q_ref, *refs):
    side = len(RING_OFFSETS)
    key_refs = refs[:side]
    value_refs = refs[side : 2 * side]
    bias_ref, res_ref, o_ref = refs[2 * side :]
    ratio = HQ // HK
    scale = 1.0 / math.sqrt(HD)
    piece = key_refs[0].shape[0]
    rows = piece // side
    for g in range(ratio):
        cols = slice(g * HD, (g + 1) * HD)
        query = q_ref[:, cols]
        masked = []
        for p in range(side):
            scores = lax.dot_general(
                query,
                key_refs[p][...],
                (((1,), (1,)), ((), ())),
                preferred_element_type=jnp.float32,
            )
            masked.append(scores * scale + bias_ref[:, p * piece : (p + 1) * piece])
        row_top = jnp.max(masked[0], axis=-1, keepdims=True)
        for p in range(1, side):
            row_top = jnp.maximum(row_top, jnp.max(masked[p], axis=-1, keepdims=True))
        weights = [jnp.exp(m - row_top) for m in masked]
        denominator = jnp.sum(weights[0], axis=-1, keepdims=True)
        for p in range(1, side):
            denominator = denominator + jnp.sum(weights[p], axis=-1, keepdims=True)
        rounded = [w.astype(jnp.bfloat16) for w in weights]
        summed = None
        for q in range(side):
            picked = jnp.concatenate(
                [rounded[p][:, q * rows : (q + 1) * rows] for p in range(side)], axis=1
            )
            part = jnp.dot(picked, value_refs[q][...], preferred_element_type=jnp.float32)
            summed = part if summed is None else summed + part
        attended = (summed / denominator).astype(jnp.bfloat16)
        o_ref[:, cols] = (
            res_ref[:, cols].astype(jnp.float32) + attended.astype(jnp.float32)
        ).astype(o_ref.dtype)


def attention(mb, turned, pieces_a, pieces_b, bias_all, residual):
    rows, width = turned.shape
    piece = pieces_a[0].shape[0]
    keys_len = bias_all.shape[2]
    group = width // HK
    piece_spec = pl.BlockSpec((piece, HD), lambda k, m: (0, k))
    grid_spec = pltpu.PrefetchScalarGridSpec(
        num_scalar_prefetch=1,
        grid=(HK,),
        in_specs=[pl.BlockSpec((rows, group), lambda k, m: (0, k))]
        + [piece_spec] * (len(pieces_a) + len(pieces_b))
        + [
            pl.BlockSpec((None, rows, keys_len), lambda k, m: (m[0], 0, 0)),
            pl.BlockSpec((rows, group), lambda k, m: (0, k)),
        ],
        out_specs=pl.BlockSpec((rows, group), lambda k, m: (0, k)),
    )
    return pl.pallas_call(
        attention_kernel,
        grid_spec=grid_spec,
        out_shape=jax.ShapeDtypeStruct((rows, width), jnp.bfloat16),
    )(mb.reshape(1), turned, *pieces_a, *pieces_b, bias_all, residual)


def local(hidden, queries, gain, key_weight, value_weight, tree_ids, branch_ids, span_order):
    section_id = lax.axis_index("section")
    shard_id = lax.axis_index("seq")
    section_count = lax.axis_size("section")
    micro_count, row_count, model_width = hidden.shape
    seq_len = tree_ids.shape[1]
    rotary_all = tree_positions(tree_ids, branch_ids)
    stored_ids = jnp.arange(seq_len, dtype=jnp.int32)
    packed_all = jnp.repeat(span_order, SPAN, axis=1) * SPAN + stored_ids % SPAN
    key_tree = by_span(tree_ids, span_order)
    key_branch = by_span(branch_ids, span_order)
    key_rotary = by_span(rotary_all, span_order)
    first_row = shard_id * row_count
    own_packed = lax.dynamic_slice_in_dim(packed_all, first_row, row_count, 1)
    own_tree = lax.dynamic_slice_in_dim(key_tree, first_row, row_count, 1)
    own_branch = lax.dynamic_slice_in_dim(key_branch, first_row, row_count, 1)
    own_rotary = lax.dynamic_slice_in_dim(key_rotary, first_row, row_count, 1)
    seq_count = lax.axis_size("seq")
    side = math.isqrt(seq_count)
    order_tree = torus_order(key_tree, shard_id, side, row_count)
    order_branch = torus_order(key_branch, shard_id, side, row_count)
    order_packed = torus_order(packed_all, shard_id, side, row_count)
    allowed = (
        (own_tree[:, :, None] == order_tree[:, None, :])
        & (order_packed[:, None, :] <= own_packed[:, :, None])
        & ((order_branch[:, None, :] == 0) | (order_branch[:, None, :] == own_branch[:, :, None]))
    )
    bias_all = jnp.where(allowed, 0.0, -jnp.inf).astype(jnp.float32)
    angles = own_rotary.astype(jnp.float32)[..., None] * frequencies()
    cos_all = jnp.cos(angles)
    sin_all = jnp.sin(angles)
    gain_row = gain[0]
    key_mat = key_weight[0]
    value_mat = value_weight[0]

    def run_layer(current, mb):
        cosine = lax.dynamic_index_in_dim(cos_all, mb, 0, keepdims=False)
        sine_part = lax.dynamic_index_in_dim(sin_all, mb, 0, keepdims=False)
        widened = current.astype(jnp.float32)
        norm_scale = lax.rsqrt(jnp.mean(widened * widened, axis=-1, keepdims=True) + 1e-05)
        normed = (widened * norm_scale * gain_row).astype(jnp.bfloat16)
        key_proj = jnp.dot(normed, key_mat, preferred_element_type=jnp.float32).reshape(
            row_count, HK, HD
        )
        key_rows = (
            rotate(key_proj, cosine[:, None, :], sine_part[:, None, :])
            .astype(jnp.bfloat16)
            .reshape(row_count, HK * HD)
        )
        value_rows = jnp.dot(normed, value_mat, preferred_element_type=jnp.float32).astype(
            jnp.bfloat16
        )
        pieces_a, pieces_b = torus_gather(key_rows, value_rows, side)
        query_local = lax.dynamic_index_in_dim(queries[0], mb, 0, keepdims=False)
        turned = (
            rotate(
                query_local.astype(jnp.float32).reshape(row_count, HQ, HD),
                cosine[:, None, :],
                sine_part[:, None, :],
            )
            .astype(jnp.bfloat16)
            .reshape(row_count, HQ * HD)
        )
        return attention(mb, turned, pieces_a, pieces_b, bias_all, current)

    tick_count = section_count + micro_count - 1

    def advance(step_id, state_pair):
        previous, outputs = state_pair
        incoming = from_behind(previous, "section", 1)
        first_mb = step_id - section_id
        active = (first_mb >= 0) & (first_mb < micro_count)
        start_at = jnp.clip(first_mb, 0, micro_count - 1)
        entering = lax.dynamic_index_in_dim(hidden, start_at, 0, keepdims=False)
        current = jnp.where(section_id == 0, entering, incoming)
        result = lax.cond(
            active,
            lambda rows: run_layer(rows, start_at),
            jnp.zeros_like,
            current,
        )
        stored = lax.dynamic_update_index_in_dim(outputs, result, start_at, 0)
        outputs = jnp.where(active, stored, outputs)
        return (result, outputs)

    empty_pass = jnp.zeros((row_count, model_width), jnp.bfloat16)
    empty_out = jnp.zeros((micro_count, row_count, model_width), jnp.bfloat16)
    final_pass, outputs = lax.fori_loop(0, tick_count, advance, (empty_pass, empty_out))
    return outputs[None]


def solution(mesh):
    placed = (
        P(None, "seq", None),
        P("section", None, "seq", None),
        P("section", None),
        P("section", None, None),
        P("section", None, None),
        P(),
        P(),
        P(),
    )
    return jax.shard_map(
        local,
        mesh=mesh,
        in_specs=placed,
        out_specs=P("section", None, "seq", None),
        check_vma=False,
    )
```

```python
import math

import jax
import jax.numpy as jnp
from jax import lax
from jax.experimental import pallas as pl
from jax.experimental.pallas import tpu as pltpu
from jax.sharding import PartitionSpec as P

HQ = 32
HK = 4
HD = 128
SPAN = 64


rope_base = 500000.0


def from_behind(value, axis, by):
    size = lax.axis_size(axis)
    pairs = [(i, i + by) for i in range(size) if 0 <= i + by < size]
    return lax.ppermute(value, axis, pairs)


def frequencies():
    exponent = jnp.arange(HD // 2, dtype=jnp.float32) * (2.0 / HD)
    return jnp.power(jnp.float32(rope_base), -exponent)


def rotate(vectors, cosine, sine_part):
    half_dim = vectors.shape[-1] // 2
    lower_half = vectors[..., :half_dim]
    upper_half = vectors[..., half_dim:]
    return jnp.concatenate(
        [
            lower_half * cosine - upper_half * sine_part,
            upper_half * cosine + lower_half * sine_part,
        ],
        axis=-1,
    )


def tree_positions(tree_ids, branch_ids):
    trees = jnp.arange(8, dtype=jnp.int32)[None, :, None]
    positions = jnp.arange(tree_ids.shape[1], dtype=jnp.int32)[None, :]
    same = tree_ids[:, None, :] == trees
    starts = jnp.sum((tree_ids[:, None, :] < trees).astype(jnp.int32), axis=2)
    chosen = jnp.sum((same & (branch_ids[:, None, :] == 1)).astype(jnp.int32), axis=2)
    own_start = jnp.sum(jnp.where(same, starts[:, :, None], 0), axis=1)
    own_chosen = jnp.sum(jnp.where(same, chosen[:, :, None], 0), axis=1)
    skipped = jnp.where(branch_ids == 2, own_chosen, 0)
    return positions - own_start - skipped


def by_span(values, span_order):
    micro_count, seq_len = values.shape
    spans = seq_len // SPAN
    blocks = values.reshape(micro_count, 1, spans, SPAN)
    picks = span_order[:, :, None] == jnp.arange(spans, dtype=jnp.int32)[None, None, :]
    chosen = jnp.where(picks[..., None], blocks, 0)
    return jnp.sum(chosen, axis=2).reshape(micro_count, seq_len)


def ring_gather(value, shift):
    ahead = shift(value, 1)
    behind = shift(value, -1)
    far = shift(ahead, 1)
    return [value, ahead, behind, far]


RING_OFFSETS = (0, -1, 1, 2)


def torus_gather(value, side):
    def shifter(along_z):
        def shift(piece, by):
            pairs = []
            for z in range(side):
                for x in range(side):
                    if along_z:
                        pairs.append((z * side + x, ((z + by) % side) * side + x))
                    else:
                        pairs.append((z * side + x, z * side + (x + by) % side))
            return lax.ppermute(piece, "seq", pairs)

        return shift

    shift_z = shifter(True)
    shift_x = shifter(False)
    rows = value.shape[0]
    width = value.shape[1] // 2
    row_a = jnp.concatenate(ring_gather(value[:, :width], shift_x), axis=0)
    pieces_a = ring_gather(row_a, shift_z)
    col_b = jnp.concatenate(ring_gather(value[:, width:], shift_z), axis=0)
    pieces_b = ring_gather(col_b, shift_x)
    return pieces_a, pieces_b


def torus_order(values, shard_id, side, rows):
    micro_count = values.shape[0]
    z = shard_id // side
    x = shard_id % side
    blocks = values.reshape(micro_count, side, side, rows)
    blocks = jnp.roll(blocks, -z, axis=1)
    blocks = jnp.roll(blocks, -x, axis=2)
    picks = [o % side for o in RING_OFFSETS]
    blocks = jnp.stack([blocks[:, p] for p in picks], axis=1)
    blocks = jnp.stack([blocks[:, :, q] for q in picks], axis=2)
    return blocks.reshape(micro_count, side * side * rows)


def attention_kernel(mb_ref, q_ref, *refs):
    side = len(RING_OFFSETS)
    key_refs = refs[:side]
    value_refs = refs[side : 2 * side]
    bias_ref, res_ref, o_ref = refs[2 * side :]
    ratio = HQ // HK
    scale = 1.0 / math.sqrt(HD)
    piece = key_refs[0].shape[0]
    rows = piece // side
    for g in range(ratio):
        cols = slice(g * HD, (g + 1) * HD)
        query = q_ref[:, cols]
        masked = []
        for p in range(side):
            scores = lax.dot_general(
                query,
                key_refs[p][...],
                (((1,), (1,)), ((), ())),
                preferred_element_type=jnp.float32,
            )
            masked.append(scores * scale + bias_ref[:, p * piece : (p + 1) * piece])
        row_top = jnp.max(masked[0], axis=-1, keepdims=True)
        for p in range(1, side):
            row_top = jnp.maximum(row_top, jnp.max(masked[p], axis=-1, keepdims=True))
        weights = [jnp.exp(m - row_top) for m in masked]
        denominator = jnp.sum(weights[0], axis=-1, keepdims=True)
        for p in range(1, side):
            denominator = denominator + jnp.sum(weights[p], axis=-1, keepdims=True)
        rounded = [w.astype(jnp.bfloat16) for w in weights]
        summed = None
        for q in range(side):
            picked = jnp.concatenate(
                [rounded[p][:, q * rows : (q + 1) * rows] for p in range(side)], axis=1
            )
            part = jnp.dot(picked, value_refs[q][...], preferred_element_type=jnp.float32)
            summed = part if summed is None else summed + part
        attended = (summed / denominator).astype(jnp.bfloat16)
        o_ref[:, cols] = (
            res_ref[:, cols].astype(jnp.float32) + attended.astype(jnp.float32)
        ).astype(o_ref.dtype)


def attention(mb, turned, pieces_a, pieces_b, bias_all, residual):
    rows, width = turned.shape
    piece = pieces_a[0].shape[0]
    keys_len = bias_all.shape[2]
    group = width // HK
    piece_spec = pl.BlockSpec((piece, HD), lambda k, m: (0, k))
    grid_spec = pltpu.PrefetchScalarGridSpec(
        num_scalar_prefetch=1,
        grid=(HK,),
        in_specs=[pl.BlockSpec((rows, group), lambda k, m: (0, k))]
        + [piece_spec] * (len(pieces_a) + len(pieces_b))
        + [
            pl.BlockSpec((None, rows, keys_len), lambda k, m: (m[0], 0, 0)),
            pl.BlockSpec((rows, group), lambda k, m: (0, k)),
        ],
        out_specs=pl.BlockSpec((rows, group), lambda k, m: (0, k)),
    )
    return pl.pallas_call(
        attention_kernel,
        grid_spec=grid_spec,
        out_shape=jax.ShapeDtypeStruct((rows, width), jnp.bfloat16),
    )(mb.reshape(1), turned, *pieces_a, *pieces_b, bias_all, residual)


def local(hidden, queries, gain, key_weight, value_weight, tree_ids, branch_ids, span_order):
    section_id = lax.axis_index("section")
    shard_id = lax.axis_index("seq")
    section_count = lax.axis_size("section")
    micro_count, row_count, model_width = hidden.shape
    seq_len = tree_ids.shape[1]
    rotary_all = tree_positions(tree_ids, branch_ids)
    stored_ids = jnp.arange(seq_len, dtype=jnp.int32)
    packed_all = jnp.repeat(span_order, SPAN, axis=1) * SPAN + stored_ids % SPAN
    key_tree = by_span(tree_ids, span_order)
    key_branch = by_span(branch_ids, span_order)
    key_rotary = by_span(rotary_all, span_order)
    first_row = shard_id * row_count
    own_packed = lax.dynamic_slice_in_dim(packed_all, first_row, row_count, 1)
    own_tree = lax.dynamic_slice_in_dim(key_tree, first_row, row_count, 1)
    own_branch = lax.dynamic_slice_in_dim(key_branch, first_row, row_count, 1)
    own_rotary = lax.dynamic_slice_in_dim(key_rotary, first_row, row_count, 1)
    seq_count = lax.axis_size("seq")
    side = math.isqrt(seq_count)
    order_tree = torus_order(key_tree, shard_id, side, row_count)
    order_branch = torus_order(key_branch, shard_id, side, row_count)
    order_packed = torus_order(packed_all, shard_id, side, row_count)
    allowed = (
        (own_tree[:, :, None] == order_tree[:, None, :])
        & (order_packed[:, None, :] <= own_packed[:, :, None])
        & ((order_branch[:, None, :] == 0) | (order_branch[:, None, :] == own_branch[:, :, None]))
    )
    bias_all = jnp.where(allowed, 0.0, -jnp.inf).astype(jnp.float32)
    angles = own_rotary.astype(jnp.float32)[..., None] * frequencies()
    cos_all = jnp.cos(angles)
    sin_all = jnp.sin(angles)
    gain_row = gain[0]
    key_mat = key_weight[0]
    value_mat = value_weight[0]
    kv_mat = jnp.concatenate([key_mat, value_mat], axis=1)

    def run_layer(current, mb):
        cosine = lax.dynamic_index_in_dim(cos_all, mb, 0, keepdims=False)
        sine_part = lax.dynamic_index_in_dim(sin_all, mb, 0, keepdims=False)
        widened = current.astype(jnp.float32)
        norm_scale = lax.rsqrt(jnp.mean(widened * widened, axis=-1, keepdims=True) + 1e-05)
        normed = (widened * norm_scale * gain_row).astype(jnp.bfloat16)
        kv_proj = jnp.dot(normed, kv_mat, preferred_element_type=jnp.float32)
        key_proj = kv_proj[:, : HK * HD].reshape(row_count, HK, HD)
        key_rows = (
            rotate(key_proj, cosine[:, None, :], sine_part[:, None, :])
            .astype(jnp.bfloat16)
            .reshape(row_count, HK * HD)
        )
        value_rows = kv_proj[:, HK * HD :].astype(jnp.bfloat16)
        kv_rows = jnp.concatenate([key_rows, value_rows], axis=1)
        pieces_a, pieces_b = torus_gather(kv_rows, side)
        query_local = lax.dynamic_index_in_dim(queries[0], mb, 0, keepdims=False)
        turned = (
            rotate(
                query_local.astype(jnp.float32).reshape(row_count, HQ, HD),
                cosine[:, None, :],
                sine_part[:, None, :],
            )
            .astype(jnp.bfloat16)
            .reshape(row_count, HQ * HD)
        )
        return attention(mb, turned, pieces_a, pieces_b, bias_all, current)

    tick_count = section_count + micro_count - 1

    def advance(step_id, state_pair):
        previous, outputs = state_pair
        incoming = from_behind(previous, "section", 1)
        first_mb = step_id - section_id
        active = (first_mb >= 0) & (first_mb < micro_count)
        start_at = jnp.clip(first_mb, 0, micro_count - 1)
        entering = lax.dynamic_index_in_dim(hidden, start_at, 0, keepdims=False)
        current = jnp.where(section_id == 0, entering, incoming)
        result = lax.cond(
            active,
            lambda rows: run_layer(rows, start_at),
            jnp.zeros_like,
            current,
        )
        stored = lax.dynamic_update_index_in_dim(outputs, result, start_at, 0)
        outputs = jnp.where(active, stored, outputs)
        return (result, outputs)

    empty_pass = jnp.zeros((row_count, model_width), jnp.bfloat16)
    empty_out = jnp.zeros((micro_count, row_count, model_width), jnp.bfloat16)
    final_pass, outputs = lax.fori_loop(0, tick_count, advance, (empty_pass, empty_out))
    return outputs[None]


def solution(mesh):
    placed = (
        P(None, "seq", None),
        P("section", None, "seq", None),
        P("section", None),
        P("section", None, None),
        P("section", None, None),
        P(),
        P(),
        P(),
    )
    return jax.shard_map(
        local,
        mesh=mesh,
        in_specs=placed,
        out_specs=P("section", None, "seq", None),
        check_vma=False,
    )
```

```python
import math

import jax
import jax.numpy as jnp
from jax import lax
from jax.experimental import pallas as pl
from jax.experimental.pallas import tpu as pltpu
from jax.sharding import PartitionSpec as P

HQ = 32
HK = 4
HD = 128
SPAN = 64


rope_base = 500000.0


def from_behind(value, axis, by):
    size = lax.axis_size(axis)
    pairs = [(i, i + by) for i in range(size) if 0 <= i + by < size]
    return lax.ppermute(value, axis, pairs)


def frequencies():
    exponent = jnp.arange(HD // 2, dtype=jnp.float32) * (2.0 / HD)
    return jnp.power(jnp.float32(rope_base), -exponent)


def rotate(vectors, cosine, sine_part):
    half_dim = vectors.shape[-1] // 2
    lower_half = vectors[..., :half_dim]
    upper_half = vectors[..., half_dim:]
    return jnp.concatenate(
        [
            lower_half * cosine - upper_half * sine_part,
            upper_half * cosine + lower_half * sine_part,
        ],
        axis=-1,
    )


def tree_positions(tree_ids, branch_ids):
    trees = jnp.arange(8, dtype=jnp.int32)[None, :, None]
    positions = jnp.arange(tree_ids.shape[1], dtype=jnp.int32)[None, :]
    same = tree_ids[:, None, :] == trees
    starts = jnp.sum((tree_ids[:, None, :] < trees).astype(jnp.int32), axis=2)
    chosen = jnp.sum((same & (branch_ids[:, None, :] == 1)).astype(jnp.int32), axis=2)
    own_start = jnp.sum(jnp.where(same, starts[:, :, None], 0), axis=1)
    own_chosen = jnp.sum(jnp.where(same, chosen[:, :, None], 0), axis=1)
    skipped = jnp.where(branch_ids == 2, own_chosen, 0)
    return positions - own_start - skipped


def by_span(values, span_order):
    micro_count, seq_len = values.shape
    spans = seq_len // SPAN
    blocks = values.reshape(micro_count, 1, spans, SPAN)
    picks = span_order[:, :, None] == jnp.arange(spans, dtype=jnp.int32)[None, None, :]
    chosen = jnp.where(picks[..., None], blocks, 0)
    return jnp.sum(chosen, axis=2).reshape(micro_count, seq_len)


def ring_gather(value, shift):
    ahead = shift(value, 1)
    behind = shift(value, -1)
    far = shift(ahead, 1)
    return [value, ahead, behind, far]


RING_OFFSETS = (0, -1, 1, 2)


def torus_gather(value, side):
    def shifter(along_z):
        def shift(piece, by):
            pairs = []
            for z in range(side):
                for x in range(side):
                    if along_z:
                        pairs.append((z * side + x, ((z + by) % side) * side + x))
                    else:
                        pairs.append((z * side + x, z * side + (x + by) % side))
            return lax.ppermute(piece, "seq", pairs)

        return shift

    shift_z = shifter(True)
    shift_x = shifter(False)
    rows = value.shape[0]
    width = value.shape[1] // 2
    row_a = jnp.concatenate(ring_gather(value[:, :width], shift_x), axis=0)
    pieces_a = ring_gather(row_a, shift_z)
    col_b = jnp.concatenate(ring_gather(value[:, width:], shift_z), axis=0)
    pieces_b = ring_gather(col_b, shift_x)
    return pieces_a, pieces_b


def torus_order(values, shard_id, side, rows):
    micro_count = values.shape[0]
    z = shard_id // side
    x = shard_id % side
    blocks = values.reshape(micro_count, side, side, rows)
    blocks = jnp.roll(blocks, -z, axis=1)
    blocks = jnp.roll(blocks, -x, axis=2)
    picks = [o % side for o in RING_OFFSETS]
    blocks = jnp.stack([blocks[:, p] for p in picks], axis=1)
    blocks = jnp.stack([blocks[:, :, q] for q in picks], axis=2)
    return blocks.reshape(micro_count, side * side * rows)


def attention_kernel(mb_ref, q_ref, *refs):
    side = len(RING_OFFSETS)
    key_refs = refs[:side]
    value_refs = refs[side : 2 * side]
    bias_ref, res_ref, o_ref = refs[2 * side :]
    ratio = HQ // HK
    scale = 1.0 / math.sqrt(HD)
    piece = key_refs[0].shape[0]
    rows = piece // side
    for g in range(ratio):
        cols = slice(g * HD, (g + 1) * HD)
        query = q_ref[:, cols]
        masked = []
        for p in range(side):
            scores = lax.dot_general(
                query,
                key_refs[p][...],
                (((1,), (1,)), ((), ())),
                preferred_element_type=jnp.float32,
            )
            masked.append(scores * scale + bias_ref[:, p * piece : (p + 1) * piece])
        row_top = jnp.max(masked[0], axis=-1, keepdims=True)
        for p in range(1, side):
            row_top = jnp.maximum(row_top, jnp.max(masked[p], axis=-1, keepdims=True))
        weights = [jnp.exp(m - row_top) for m in masked]
        denominator = jnp.sum(weights[0], axis=-1, keepdims=True)
        for p in range(1, side):
            denominator = denominator + jnp.sum(weights[p], axis=-1, keepdims=True)
        rounded = [w.astype(jnp.bfloat16) for w in weights]
        summed = None
        for q in range(side):
            picked = jnp.concatenate(
                [rounded[p][:, q * rows : (q + 1) * rows] for p in range(side)], axis=1
            )
            part = jnp.dot(picked, value_refs[q][...], preferred_element_type=jnp.float32)
            summed = part if summed is None else summed + part
        attended = (summed / denominator).astype(jnp.bfloat16)
        o_ref[:, cols] = (
            res_ref[:, cols].astype(jnp.float32) + attended.astype(jnp.float32)
        ).astype(o_ref.dtype)


def attention(mb, turned, pieces_a, pieces_b, bias_all, residual):
    rows, width = turned.shape
    piece = pieces_a[0].shape[0]
    keys_len = bias_all.shape[2]
    group = width // HK
    piece_spec = pl.BlockSpec((piece, HD), lambda k, m: (0, k))
    grid_spec = pltpu.PrefetchScalarGridSpec(
        num_scalar_prefetch=1,
        grid=(HK,),
        in_specs=[pl.BlockSpec((rows, group), lambda k, m: (0, k))]
        + [piece_spec] * (len(pieces_a) + len(pieces_b))
        + [
            pl.BlockSpec((None, rows, keys_len), lambda k, m: (m[0], 0, 0)),
            pl.BlockSpec((rows, group), lambda k, m: (0, k)),
        ],
        out_specs=pl.BlockSpec((rows, group), lambda k, m: (0, k)),
    )
    return pl.pallas_call(
        attention_kernel,
        grid_spec=grid_spec,
        out_shape=jax.ShapeDtypeStruct((rows, width), jnp.bfloat16),
    )(mb.reshape(1), turned, *pieces_a, *pieces_b, bias_all, residual)


def local(hidden, queries, gain, key_weight, value_weight, tree_ids, branch_ids, span_order):
    section_id = lax.axis_index("section")
    shard_id = lax.axis_index("seq")
    section_count = lax.axis_size("section")
    micro_count, row_count, model_width = hidden.shape
    seq_len = tree_ids.shape[1]
    rotary_all = tree_positions(tree_ids, branch_ids)
    stored_ids = jnp.arange(seq_len, dtype=jnp.int32)
    packed_all = jnp.repeat(span_order, SPAN, axis=1) * SPAN + stored_ids % SPAN
    key_tree = by_span(tree_ids, span_order)
    key_branch = by_span(branch_ids, span_order)
    key_rotary = by_span(rotary_all, span_order)
    first_row = shard_id * row_count
    own_packed = lax.dynamic_slice_in_dim(packed_all, first_row, row_count, 1)
    own_tree = lax.dynamic_slice_in_dim(key_tree, first_row, row_count, 1)
    own_branch = lax.dynamic_slice_in_dim(key_branch, first_row, row_count, 1)
    own_rotary = lax.dynamic_slice_in_dim(key_rotary, first_row, row_count, 1)
    seq_count = lax.axis_size("seq")
    side = math.isqrt(seq_count)
    order_tree = torus_order(key_tree, shard_id, side, row_count)
    order_branch = torus_order(key_branch, shard_id, side, row_count)
    order_packed = torus_order(packed_all, shard_id, side, row_count)
    allowed = (
        (own_tree[:, :, None] == order_tree[:, None, :])
        & (order_packed[:, None, :] <= own_packed[:, :, None])
        & ((order_branch[:, None, :] == 0) | (order_branch[:, None, :] == own_branch[:, :, None]))
    )
    bias_all = jnp.where(allowed, 0.0, -jnp.inf).astype(jnp.float32)
    angles = own_rotary.astype(jnp.float32)[..., None] * frequencies()
    cos_all = jnp.cos(angles)
    sin_all = jnp.sin(angles)
    gain_row = gain[0]
    key_mat = key_weight[0]
    value_mat = value_weight[0]
    kv_mat = jnp.concatenate([key_mat, value_mat], axis=1)

    def run_layer(current, mb):
        cosine = lax.dynamic_index_in_dim(cos_all, mb, 0, keepdims=False)
        sine_part = lax.dynamic_index_in_dim(sin_all, mb, 0, keepdims=False)
        widened = current.astype(jnp.float32)
        norm_scale = lax.rsqrt(jnp.mean(widened * widened, axis=-1, keepdims=True) + 1e-05)
        normed = (widened * norm_scale * gain_row).astype(jnp.bfloat16)
        kv_proj = jnp.dot(normed, kv_mat, preferred_element_type=jnp.float32)
        key_proj = kv_proj[:, : HK * HD].reshape(row_count, HK, HD)
        key_rows = (
            rotate(key_proj, cosine[:, None, :], sine_part[:, None, :])
            .astype(jnp.bfloat16)
            .reshape(row_count, HK * HD)
        )
        value_rows = kv_proj[:, HK * HD :].astype(jnp.bfloat16)
        kv_rows = jnp.concatenate([key_rows, value_rows], axis=1)
        pieces_a, pieces_b = torus_gather(kv_rows, side)
        query_local = lax.dynamic_index_in_dim(queries[0], mb, 0, keepdims=False)
        turned = (
            rotate(
                query_local.astype(jnp.float32).reshape(row_count, HQ, HD),
                cosine[:, None, :],
                sine_part[:, None, :],
            )
            .astype(jnp.bfloat16)
            .reshape(row_count, HQ * HD)
        )
        return attention(mb, turned, pieces_a, pieces_b, bias_all, current)

    tick_count = section_count + micro_count - 1

    def advance(step_id, state_pair):
        previous, outputs = state_pair
        incoming = from_behind(previous, "section", 1)
        first_mb = step_id - section_id
        active = (first_mb >= 0) & (first_mb < micro_count)
        start_at = jnp.clip(first_mb, 0, micro_count - 1)
        entering = lax.dynamic_index_in_dim(hidden, start_at, 0, keepdims=False)
        current = jnp.where(section_id == 0, entering, incoming)
        def busy(operands):
            rows, kept = operands
            computed = run_layer(rows, start_at)
            return computed, lax.dynamic_update_index_in_dim(kept, computed, start_at, 0)

        def idle(operands):
            rows, kept = operands
            return jnp.zeros_like(rows), kept

        return lax.cond(active, busy, idle, (current, outputs))

    empty_pass = jnp.zeros((row_count, model_width), jnp.bfloat16)
    empty_out = jnp.zeros((micro_count, row_count, model_width), jnp.bfloat16)
    final_pass, outputs = lax.fori_loop(0, tick_count, advance, (empty_pass, empty_out))
    return outputs[None]


def solution(mesh):
    placed = (
        P(None, "seq", None),
        P("section", None, "seq", None),
        P("section", None),
        P("section", None, None),
        P("section", None, None),
        P(),
        P(),
        P(),
    )
    return jax.shard_map(
        local,
        mesh=mesh,
        in_specs=placed,
        out_specs=P("section", None, "seq", None),
        check_vma=False,
    )
```

```python
import math

import jax
import jax.numpy as jnp
from jax import lax
from jax.experimental import pallas as pl
from jax.experimental.pallas import tpu as pltpu
from jax.sharding import PartitionSpec as P

HQ = 32
HK = 4
HD = 128
SPAN = 64


rope_base = 500000.0


def from_behind(value, axis, by):
    size = lax.axis_size(axis)
    pairs = [(i, i + by) for i in range(size) if 0 <= i + by < size]
    return lax.ppermute(value, axis, pairs)


def frequencies():
    exponent = jnp.arange(HD // 2, dtype=jnp.float32) * (2.0 / HD)
    return jnp.power(jnp.float32(rope_base), -exponent)


def rotate(vectors, cosine, sine_part):
    half_dim = vectors.shape[-1] // 2
    lower_half = vectors[..., :half_dim]
    upper_half = vectors[..., half_dim:]
    return jnp.concatenate(
        [
            lower_half * cosine - upper_half * sine_part,
            upper_half * cosine + lower_half * sine_part,
        ],
        axis=-1,
    )


def tree_positions(tree_ids, branch_ids):
    trees = jnp.arange(8, dtype=jnp.int32)[None, :, None]
    positions = jnp.arange(tree_ids.shape[1], dtype=jnp.int32)[None, :]
    same = tree_ids[:, None, :] == trees
    starts = jnp.sum((tree_ids[:, None, :] < trees).astype(jnp.int32), axis=2)
    chosen = jnp.sum((same & (branch_ids[:, None, :] == 1)).astype(jnp.int32), axis=2)
    own_start = jnp.sum(jnp.where(same, starts[:, :, None], 0), axis=1)
    own_chosen = jnp.sum(jnp.where(same, chosen[:, :, None], 0), axis=1)
    skipped = jnp.where(branch_ids == 2, own_chosen, 0)
    return positions - own_start - skipped


def by_span(values, span_order):
    micro_count, seq_len = values.shape
    spans = seq_len // SPAN
    blocks = values.reshape(micro_count, 1, spans, SPAN)
    picks = span_order[:, :, None] == jnp.arange(spans, dtype=jnp.int32)[None, None, :]
    chosen = jnp.where(picks[..., None], blocks, 0)
    return jnp.sum(chosen, axis=2).reshape(micro_count, seq_len)


def ring_gather(value, shift):
    ahead = shift(value, 1)
    behind = shift(value, -1)
    far = shift(ahead, 1)
    return [value, ahead, behind, far]


RING_OFFSETS = (0, -1, 1, 2)


def torus_gather(value, side):
    def shifter(along_z):
        def shift(piece, by):
            pairs = []
            for z in range(side):
                for x in range(side):
                    if along_z:
                        pairs.append((z * side + x, ((z + by) % side) * side + x))
                    else:
                        pairs.append((z * side + x, z * side + (x + by) % side))
            return lax.ppermute(piece, "seq", pairs)

        return shift

    shift_z = shifter(True)
    shift_x = shifter(False)
    rows = value.shape[0]
    width = value.shape[1] // 2
    row_a = jnp.concatenate(ring_gather(value[:, :width], shift_x), axis=0)
    pieces_a = ring_gather(row_a, shift_z)
    col_b = jnp.concatenate(ring_gather(value[:, width:], shift_z), axis=0)
    pieces_b = ring_gather(col_b, shift_x)
    return pieces_a, pieces_b


def torus_order(values, shard_id, side, rows):
    micro_count = values.shape[0]
    z = shard_id // side
    x = shard_id % side
    blocks = values.reshape(micro_count, side, side, rows)
    blocks = jnp.roll(blocks, -z, axis=1)
    blocks = jnp.roll(blocks, -x, axis=2)
    picks = [o % side for o in RING_OFFSETS]
    blocks = jnp.stack([blocks[:, p] for p in picks], axis=1)
    blocks = jnp.stack([blocks[:, :, q] for q in picks], axis=2)
    return blocks.reshape(micro_count, side * side * rows)


def attention_kernel(mb_ref, q_ref, *refs):
    side = len(RING_OFFSETS)
    key_refs = refs[:side]
    value_refs = refs[side : 2 * side]
    bias_ref, res_ref, o_ref = refs[2 * side :]
    ratio = HQ // HK
    scale = 1.0 / math.sqrt(HD)
    piece = key_refs[0].shape[0]
    rows = piece // side
    for g in range(ratio):
        cols = slice(g * HD, (g + 1) * HD)
        query = q_ref[:, cols]
        masked = []
        for p in range(side):
            scores = lax.dot_general(
                query,
                key_refs[p][...],
                (((1,), (1,)), ((), ())),
                preferred_element_type=jnp.float32,
            )
            masked.append(scores * scale + bias_ref[:, p * piece : (p + 1) * piece])
        row_top = jnp.max(masked[0], axis=-1, keepdims=True)
        for p in range(1, side):
            row_top = jnp.maximum(row_top, jnp.max(masked[p], axis=-1, keepdims=True))
        weights = [jnp.exp(m - row_top) for m in masked]
        denominator = jnp.sum(weights[0], axis=-1, keepdims=True)
        for p in range(1, side):
            denominator = denominator + jnp.sum(weights[p], axis=-1, keepdims=True)
        rounded = [w.astype(jnp.bfloat16) for w in weights]
        summed = None
        for q in range(side):
            picked = jnp.concatenate(
                [rounded[p][:, q * rows : (q + 1) * rows] for p in range(side)], axis=1
            )
            part = jnp.dot(picked, value_refs[q][...], preferred_element_type=jnp.float32)
            summed = part if summed is None else summed + part
        attended = (summed / denominator).astype(jnp.bfloat16)
        o_ref[:, cols] = (
            res_ref[:, cols].astype(jnp.float32) + attended.astype(jnp.float32)
        ).astype(o_ref.dtype)


def attention(mb, turned, pieces_a, pieces_b, bias_all, residual):
    rows, width = turned.shape
    piece = pieces_a[0].shape[0]
    keys_len = bias_all.shape[2]
    group = width // HK
    piece_spec = pl.BlockSpec((piece, HD), lambda k, m: (0, k))
    grid_spec = pltpu.PrefetchScalarGridSpec(
        num_scalar_prefetch=1,
        grid=(HK,),
        in_specs=[pl.BlockSpec((rows, group), lambda k, m: (0, k))]
        + [piece_spec] * (len(pieces_a) + len(pieces_b))
        + [
            pl.BlockSpec((None, rows, keys_len), lambda k, m: (m[0], 0, 0)),
            pl.BlockSpec((rows, group), lambda k, m: (0, k)),
        ],
        out_specs=pl.BlockSpec((rows, group), lambda k, m: (0, k)),
    )
    return pl.pallas_call(
        attention_kernel,
        grid_spec=grid_spec,
        out_shape=jax.ShapeDtypeStruct((rows, width), jnp.bfloat16),
    )(mb.reshape(1), turned, *pieces_a, *pieces_b, bias_all, residual)


def local(hidden, queries, gain, key_weight, value_weight, tree_ids, branch_ids, span_order):
    section_id = lax.axis_index("section")
    shard_id = lax.axis_index("seq")
    section_count = lax.axis_size("section")
    micro_count, row_count, model_width = hidden.shape
    seq_len = tree_ids.shape[1]
    rotary_all = tree_positions(tree_ids, branch_ids)
    stored_ids = jnp.arange(seq_len, dtype=jnp.int32)
    packed_all = jnp.repeat(span_order, SPAN, axis=1) * SPAN + stored_ids % SPAN
    key_tree = by_span(tree_ids, span_order)
    key_branch = by_span(branch_ids, span_order)
    key_rotary = by_span(rotary_all, span_order)
    first_row = shard_id * row_count
    own_packed = lax.dynamic_slice_in_dim(packed_all, first_row, row_count, 1)
    own_tree = lax.dynamic_slice_in_dim(key_tree, first_row, row_count, 1)
    own_branch = lax.dynamic_slice_in_dim(key_branch, first_row, row_count, 1)
    own_rotary = lax.dynamic_slice_in_dim(key_rotary, first_row, row_count, 1)
    seq_count = lax.axis_size("seq")
    side = math.isqrt(seq_count)
    order_tree = torus_order(key_tree, shard_id, side, row_count)
    order_branch = torus_order(key_branch, shard_id, side, row_count)
    order_packed = torus_order(packed_all, shard_id, side, row_count)
    allowed = (
        (own_tree[:, :, None] == order_tree[:, None, :])
        & (order_packed[:, None, :] <= own_packed[:, :, None])
        & ((order_branch[:, None, :] == 0) | (order_branch[:, None, :] == own_branch[:, :, None]))
    )
    bias_all = jnp.where(allowed, 0.0, -jnp.inf).astype(jnp.float32)
    angles = own_rotary.astype(jnp.float32)[..., None] * frequencies()
    cos_all = jnp.cos(angles)
    sin_all = jnp.sin(angles)
    gain_row = gain[0]
    key_mat = key_weight[0]
    value_mat = value_weight[0]
    kv_mat = jnp.concatenate([key_mat, value_mat], axis=1)

    def run_layer(current, mb):
        cosine = lax.dynamic_index_in_dim(cos_all, mb, 0, keepdims=False)
        sine_part = lax.dynamic_index_in_dim(sin_all, mb, 0, keepdims=False)
        widened = current.astype(jnp.float32)
        norm_scale = lax.rsqrt(jnp.mean(widened * widened, axis=-1, keepdims=True) + 1e-05)
        normed = (widened * norm_scale * gain_row).astype(jnp.bfloat16)
        kv_proj = jnp.dot(normed, kv_mat, preferred_element_type=jnp.float32)
        key_proj = kv_proj[:, : HK * HD].reshape(row_count, HK, HD)
        key_rows = (
            rotate(key_proj, cosine[:, None, :], sine_part[:, None, :])
            .astype(jnp.bfloat16)
            .reshape(row_count, HK * HD)
        )
        value_rows = kv_proj[:, HK * HD :].astype(jnp.bfloat16)
        kv_rows = jnp.concatenate([key_rows, value_rows], axis=1)
        pieces_a, pieces_b = torus_gather(kv_rows, side)
        query_local = lax.dynamic_index_in_dim(queries[0], mb, 0, keepdims=False)
        turned = (
            rotate(
                query_local.astype(jnp.float32).reshape(row_count, HQ, HD),
                cosine[:, None, :],
                sine_part[:, None, :],
            )
            .astype(jnp.bfloat16)
            .reshape(row_count, HQ * HD)
        )
        return attention(mb, turned, pieces_a, pieces_b, bias_all, current)

    tick_count = section_count + micro_count - 1

    def advance(step_id, state_pair):
        previous, outputs = state_pair
        incoming = from_behind(previous, "section", 1)
        first_mb = step_id - section_id
        active = (first_mb >= 0) & (first_mb < micro_count)
        start_at = jnp.clip(first_mb, 0, micro_count - 1)
        entering = lax.dynamic_index_in_dim(hidden, start_at, 0, keepdims=False)
        current = jnp.where(section_id == 0, entering, incoming)
        result = lax.cond(
            active,
            lambda rows: run_layer(rows, start_at),
            lambda rows: rows,
            current,
        )
        stored = lax.dynamic_update_index_in_dim(outputs, result, start_at, 0)
        outputs = jnp.where(active, stored, outputs)
        return (result, outputs)

    empty_pass = jnp.zeros((row_count, model_width), jnp.bfloat16)
    empty_out = jnp.zeros((micro_count, row_count, model_width), jnp.bfloat16)
    final_pass, outputs = lax.fori_loop(0, tick_count, advance, (empty_pass, empty_out))
    return outputs[None]


def solution(mesh):
    placed = (
        P(None, "seq", None),
        P("section", None, "seq", None),
        P("section", None),
        P("section", None, None),
        P("section", None, None),
        P(),
        P(),
        P(),
    )
    return jax.shard_map(
        local,
        mesh=mesh,
        in_specs=placed,
        out_specs=P("section", None, "seq", None),
        check_vma=False,
    )
```

```python
import math

import jax
import jax.numpy as jnp
from jax import lax
from jax.experimental import pallas as pl
from jax.experimental.pallas import tpu as pltpu
from jax.sharding import PartitionSpec as P

HQ = 32
HK = 4
HD = 128
SPAN = 64


rope_base = 500000.0


def from_behind(value, axis, by):
    size = lax.axis_size(axis)
    pairs = [(i, i + by) for i in range(size) if 0 <= i + by < size]
    return lax.ppermute(value, axis, pairs)


def frequencies():
    exponent = jnp.arange(HD // 2, dtype=jnp.float32) * (2.0 / HD)
    return jnp.power(jnp.float32(rope_base), -exponent)


def rotate(vectors, cosine, sine_part):
    half_dim = vectors.shape[-1] // 2
    lower_half = vectors[..., :half_dim]
    upper_half = vectors[..., half_dim:]
    return jnp.concatenate(
        [
            lower_half * cosine - upper_half * sine_part,
            upper_half * cosine + lower_half * sine_part,
        ],
        axis=-1,
    )


def tree_positions(tree_ids, branch_ids):
    trees = jnp.arange(8, dtype=jnp.int32)[None, :, None]
    positions = jnp.arange(tree_ids.shape[1], dtype=jnp.int32)[None, :]
    same = tree_ids[:, None, :] == trees
    starts = jnp.sum((tree_ids[:, None, :] < trees).astype(jnp.int32), axis=2)
    chosen = jnp.sum((same & (branch_ids[:, None, :] == 1)).astype(jnp.int32), axis=2)
    own_start = jnp.sum(jnp.where(same, starts[:, :, None], 0), axis=1)
    own_chosen = jnp.sum(jnp.where(same, chosen[:, :, None], 0), axis=1)
    skipped = jnp.where(branch_ids == 2, own_chosen, 0)
    return positions - own_start - skipped


def by_span(values, span_order):
    micro_count, seq_len = values.shape
    spans = seq_len // SPAN
    blocks = values.reshape(micro_count, 1, spans, SPAN)
    picks = span_order[:, :, None] == jnp.arange(spans, dtype=jnp.int32)[None, None, :]
    chosen = jnp.where(picks[..., None], blocks, 0)
    return jnp.sum(chosen, axis=2).reshape(micro_count, seq_len)


def ring_gather(value, shift):
    ahead = shift(value, 1)
    behind = shift(value, -1)
    far = shift(ahead, 1)
    return [value, ahead, behind, far]


RING_OFFSETS = (0, -1, 1, 2)


def torus_gather(value, side):
    def shifter(along_z):
        def shift(piece, by):
            pairs = []
            for z in range(side):
                for x in range(side):
                    if along_z:
                        pairs.append((z * side + x, ((z + by) % side) * side + x))
                    else:
                        pairs.append((z * side + x, z * side + (x + by) % side))
            return lax.ppermute(piece, "seq", pairs)

        return shift

    shift_z = shifter(True)
    shift_x = shifter(False)
    rows = value.shape[0]
    width = value.shape[1] // 2
    row_a = jnp.concatenate(ring_gather(value[:, :width], shift_x), axis=0)
    pieces_a = ring_gather(row_a, shift_z)
    col_b = jnp.concatenate(ring_gather(value[:, width:], shift_z), axis=0)
    pieces_b = ring_gather(col_b, shift_x)
    return pieces_a, pieces_b


def torus_order(values, shard_id, side, rows):
    micro_count = values.shape[0]
    z = shard_id // side
    x = shard_id % side
    blocks = values.reshape(micro_count, side, side, rows)
    blocks = jnp.roll(blocks, -z, axis=1)
    blocks = jnp.roll(blocks, -x, axis=2)
    picks = [o % side for o in RING_OFFSETS]
    blocks = jnp.stack([blocks[:, p] for p in picks], axis=1)
    blocks = jnp.stack([blocks[:, :, q] for q in picks], axis=2)
    return blocks.reshape(micro_count, side * side * rows)


def attention_kernel(mb_ref, q_ref, *refs):
    side = len(RING_OFFSETS)
    key_refs = refs[:side]
    value_refs = refs[side : 2 * side]
    bias_ref, res_ref, o_ref = refs[2 * side :]
    ratio = HQ // HK
    scale = 1.0 / math.sqrt(HD)
    piece = key_refs[0].shape[0]
    rows = piece // side
    for g in range(ratio):
        cols = slice(g * HD, (g + 1) * HD)
        query = q_ref[:, cols]
        masked = []
        for p in range(side):
            scores = lax.dot_general(
                query,
                key_refs[p][...],
                (((1,), (1,)), ((), ())),
                preferred_element_type=jnp.float32,
            )
            masked.append(scores * scale + bias_ref[:, p * piece : (p + 1) * piece])
        row_top = jnp.max(masked[0], axis=-1, keepdims=True)
        for p in range(1, side):
            row_top = jnp.maximum(row_top, jnp.max(masked[p], axis=-1, keepdims=True))
        weights = [jnp.exp(m - row_top) for m in masked]
        denominator = jnp.sum(weights[0], axis=-1, keepdims=True)
        for p in range(1, side):
            denominator = denominator + jnp.sum(weights[p], axis=-1, keepdims=True)
        rounded = [w.astype(jnp.bfloat16) for w in weights]
        summed = None
        for q in range(side):
            picked = jnp.concatenate(
                [rounded[p][:, q * rows : (q + 1) * rows] for p in range(side)], axis=1
            )
            part = jnp.dot(picked, value_refs[q][...], preferred_element_type=jnp.float32)
            summed = part if summed is None else summed + part
        attended = (summed / denominator).astype(jnp.bfloat16)
        o_ref[:, cols] = (
            res_ref[:, cols].astype(jnp.float32) + attended.astype(jnp.float32)
        ).astype(o_ref.dtype)


def attention(mb, turned, pieces_a, pieces_b, bias_all, residual):
    rows, width = turned.shape
    piece = pieces_a[0].shape[0]
    keys_len = bias_all.shape[2]
    group = width // HK
    piece_spec = pl.BlockSpec((piece, HD), lambda k, m: (0, k))
    grid_spec = pltpu.PrefetchScalarGridSpec(
        num_scalar_prefetch=1,
        grid=(HK,),
        in_specs=[pl.BlockSpec((rows, group), lambda k, m: (0, k))]
        + [piece_spec] * (len(pieces_a) + len(pieces_b))
        + [
            pl.BlockSpec((None, rows, keys_len), lambda k, m: (m[0], 0, 0)),
            pl.BlockSpec((rows, group), lambda k, m: (0, k)),
        ],
        out_specs=pl.BlockSpec((rows, group), lambda k, m: (0, k)),
    )
    return pl.pallas_call(
        attention_kernel,
        grid_spec=grid_spec,
        out_shape=jax.ShapeDtypeStruct((rows, width), jnp.bfloat16),
    )(mb.reshape(1), turned, *pieces_a, *pieces_b, bias_all, residual)


def local(hidden, queries, gain, key_weight, value_weight, tree_ids, branch_ids, span_order):
    section_id = lax.axis_index("section")
    shard_id = lax.axis_index("seq")
    section_count = lax.axis_size("section")
    micro_count, row_count, model_width = hidden.shape
    seq_len = tree_ids.shape[1]
    rotary_all = tree_positions(tree_ids, branch_ids)
    stored_ids = jnp.arange(seq_len, dtype=jnp.int32)
    packed_all = jnp.repeat(span_order, SPAN, axis=1) * SPAN + stored_ids % SPAN
    key_tree = by_span(tree_ids, span_order)
    key_branch = by_span(branch_ids, span_order)
    key_rotary = by_span(rotary_all, span_order)
    first_row = shard_id * row_count
    own_packed = lax.dynamic_slice_in_dim(packed_all, first_row, row_count, 1)
    own_tree = lax.dynamic_slice_in_dim(key_tree, first_row, row_count, 1)
    own_branch = lax.dynamic_slice_in_dim(key_branch, first_row, row_count, 1)
    own_rotary = lax.dynamic_slice_in_dim(key_rotary, first_row, row_count, 1)
    seq_count = lax.axis_size("seq")
    side = math.isqrt(seq_count)
    order_tree = torus_order(key_tree, shard_id, side, row_count)
    order_branch = torus_order(key_branch, shard_id, side, row_count)
    order_packed = torus_order(packed_all, shard_id, side, row_count)
    allowed = (
        (own_tree[:, :, None] == order_tree[:, None, :])
        & (order_packed[:, None, :] <= own_packed[:, :, None])
        & ((order_branch[:, None, :] == 0) | (order_branch[:, None, :] == own_branch[:, :, None]))
    )
    bias_all = jnp.where(allowed, 0.0, -jnp.inf).astype(jnp.float32)
    angles = own_rotary.astype(jnp.float32)[..., None] * frequencies()
    cos_all = jnp.cos(angles)
    sin_all = jnp.sin(angles)
    gain_row = gain[0]
    key_mat = key_weight[0]
    value_mat = value_weight[0]
    kv_mat = jnp.concatenate([key_mat, value_mat], axis=1)

    def run_layer(current, mb):
        cosine = lax.dynamic_index_in_dim(cos_all, mb, 0, keepdims=False)
        sine_part = lax.dynamic_index_in_dim(sin_all, mb, 0, keepdims=False)
        widened = current.astype(jnp.float32)
        norm_scale = lax.rsqrt(jnp.mean(widened * widened, axis=-1, keepdims=True) + 1e-05)
        normed = (widened * norm_scale * gain_row).astype(jnp.bfloat16)
        kv_proj = jnp.dot(normed, kv_mat, preferred_element_type=jnp.float32)
        key_proj = kv_proj[:, : HK * HD].reshape(row_count, HK, HD)
        key_rows = (
            rotate(key_proj, cosine[:, None, :], sine_part[:, None, :])
            .astype(jnp.bfloat16)
            .reshape(row_count, HK * HD)
        )
        value_rows = kv_proj[:, HK * HD :].astype(jnp.bfloat16)
        kv_rows = jnp.concatenate([key_rows, value_rows], axis=1)
        pieces_a, pieces_b = torus_gather(kv_rows, side)
        query_local = lax.dynamic_index_in_dim(queries[0], mb, 0, keepdims=False)
        turned = (
            rotate(
                query_local.astype(jnp.float32).reshape(row_count, HQ, HD),
                cosine[:, None, :],
                sine_part[:, None, :],
            )
            .astype(jnp.bfloat16)
            .reshape(row_count, HQ * HD)
        )
        return attention(mb, turned, pieces_a, pieces_b, bias_all, current)

    tick_count = section_count + micro_count - 1

    def advance(step_id, state_pair):
        previous, outputs = state_pair
        incoming = from_behind(previous, "section", 1)
        first_mb = step_id - section_id
        active = (first_mb >= 0) & (first_mb < micro_count)
        start_at = jnp.clip(first_mb, 0, micro_count - 1)
        entering = lax.dynamic_index_in_dim(hidden, start_at, 0, keepdims=False)
        current = jnp.where(section_id == 0, entering, incoming)
        def busy(operands):
            rows, kept = operands
            computed = run_layer(rows, start_at)
            return computed, lax.dynamic_update_index_in_dim(kept, computed, start_at, 0)

        return lax.cond(active, busy, lambda operands: operands, (current, outputs))

    empty_pass = jnp.zeros((row_count, model_width), jnp.bfloat16)
    empty_out = jnp.zeros((micro_count, row_count, model_width), jnp.bfloat16)
    final_pass, outputs = lax.fori_loop(0, tick_count, advance, (empty_pass, empty_out))
    return outputs[None]


def solution(mesh):
    placed = (
        P(None, "seq", None),
        P("section", None, "seq", None),
        P("section", None),
        P("section", None, None),
        P("section", None, None),
        P(),
        P(),
        P(),
    )
    return jax.shard_map(
        local,
        mesh=mesh,
        in_specs=placed,
        out_specs=P("section", None, "seq", None),
        check_vma=False,
    )
```
